512 devices in a mesh: sub: 128 (over z, y, core), harm: 4 (over x).
Axes of the slice: x: 4, y: 8, z: 8, core: 2. Of those that a mesh axis runs over, the one named last changes fastest.
Arguments:
- lengths: int32 [384], P('sub'), may hold values from 128 to 1024, as said below
- owners: int32 [384, 1], P('sub'), may hold values from 0 to 127, as said below
- front_inverse: bfloat16 [384, 1024, 1024], P('sub', 'harm'), may hold values from -0.1875 to 0.1875
- coupling: bfloat16 [384, 1024, 768], P('sub', 'harm'), may hold values from -0.1875 to 0.1875
- stiffness: bfloat16 [384, 768, 768], P('sub', 'harm'), may hold values from -0.21875 to 0.21875
- displacement: bfloat16 [128, 32, 768], P('sub', 'harm'), may hold values from -6 to 6
- forcing: float32 [128, 32, 768], P('sub', 'harm'), may hold values from -6 to 6
- lumped_mass: float32 [128, 768], P('sub'), may hold values from 0.2 to 2
- damping: float32 [128, 768], P('sub'), may hold values from 0.1 to 1.5
Outputs:
- interior: bfloat16 [384, 32, 1024], P('sub', None, 'harm')
- residual: float32 [128, 32, 768], P('sub', 'harm')
- modes: bfloat16 [384, 1024, 768], P('sub', 'harm')
The draws below stay inside these ranges and needn't reach their ends.
Inputs may be any that keep to these rules, and one draw needn't show every extreme that they name: `lengths`: live interior front rows of each substructure, which are its first rows; some substructure has all 1024. `owners`: substructure k lies on sub index k // 3; on every sub index d, the first 2 of its 3 substructures are attached to block (d + 64) mod 128, the third to a block of uneven popularity; every interface block has at least one substructure.
All inputs are finite; a program needn't handle non-finite values.
Results may differ from the reference program's by a relative error of at most 0.008.
Values may be sent and summed in bfloat16 or wider, within the bound.
No kernel may reach another device: no remote copies, remote signals or barrier semaphores. Data moves between devices by JAX's collectives and lax.ppermute only.
A program may use at most 64 MiB of HBM per device.

```python
import math
import jax
import jax.numpy as jnp
from jax import lax

SUB_DEV = 3
F = 1024
NB = 768
H = 16
SUBS = 384
NOWN = 128


def draw_lengths(key, part):
    first = jax.random.fold_in(key, 11)
    second = jax.random.fold_in(key, 23)
    spread = jax.random.randint(first, (SUBS,), 0, 64)
    base = F // 8 + (F - F // 8) * spread * spread // 4095
    chosen = jax.random.randint(second, (), 0, SUBS)
    return jnp.where(jnp.arange(SUBS) == chosen, F, base).astype(jnp.int32)


def draw_owners(key, part):
    first = jax.random.fold_in(key, 31)
    second = jax.random.fold_in(key, 37)
    third = jax.random.fold_in(key, 41)
    index = jnp.arange(SUBS, dtype=jnp.int32)
    device = index // SUB_DEV
    slot = index % SUB_DEV
    far = (device + NOWN // 2) % NOWN
    left = jax.random.randint(first, (SUBS,), 0, NOWN)
    right = jax.random.randint(second, (SUBS,), 0, NOWN)
    relabel = jax.random.permutation(third, NOWN).astype(jnp.int32)
    skewed = relabel[left * right // NOWN]
    chosen = jnp.where(slot < (SUB_DEV + 1) // 2, far, skewed)
    return chosen.astype(jnp.int32).reshape(SUBS, 1)


def levels(rng, dims, cuts, least, top_value):
    gain = 1.0
    for dim, blocks in cuts:
        draws = jax.random.uniform(jax.random.fold_in(jax.random.fold_in(rng, 6), dim), (blocks,), jnp.float32, least / len(cuts), top_value / len(cuts))
        gain = gain * jnp.repeat(jnp.exp(draws), dims[dim] // blocks).reshape((-1,) + (1,) * (len(dims) - 1 - dim))
    return gain


def centred(rng, extent, width, bound, cuts=(), kind=jnp.bfloat16):
    entries = jax.random.normal(rng, extent, jnp.float32) * width
    if len(cuts) > 0:
        entries = levels(rng, extent, cuts, -0.22, 0.18) * entries
    return jnp.clip(entries, min=-bound, max=bound).astype(kind)


def setup_inputs(seed: int = 0) -> dict:
    arg_keys = jax.random.split(jax.random.key(seed), 10)
    lengths = draw_lengths(jax.random.fold_in(arg_keys[9], 71), 0)
    owners = draw_owners(jax.random.fold_in(arg_keys[9], 71), 0)
    front_inverse = centred(arg_keys[2], (SUBS, F, F), F ** -0.5, 0.1875, ((0, 128), (1, 4)))
    coupling = centred(arg_keys[3], (SUBS, F, NB), F ** -0.5, 0.1875, ((0, 128), (1, 4)))
    stiffness = centred(arg_keys[4], (SUBS, NB, NB), NB ** -0.5, 0.21875, ((0, 128), (1, 4)))
    displacement = centred(arg_keys[5], (NOWN, 2 * H, NB), 1.0, 6.0, ((0, 128), (1, 4)))
    forcing = centred(arg_keys[6], (NOWN, 2 * H, NB), 1.0, 6.0, ((0, 128), (1, 4)), jnp.float32)
    lumped_mass = jnp.clip(jnp.exp(math.log(2.0) - 2.3025851 * jax.random.uniform(arg_keys[7], (NOWN, NB), jnp.float32) ** levels(arg_keys[7], (NOWN, NB), ((0, 128),), -0.2, 0.2)), 0.2, 2.0)
    damping = jnp.clip(jnp.exp(math.log(1.5) - 2.7080502 * jax.random.uniform(arg_keys[8], (NOWN, NB), jnp.float32) ** levels(arg_keys[8], (NOWN, NB), ((0, 128),), -0.2, 0.2)), 0.1, 1.5)
    return dict(lengths=lengths, owners=owners, front_inverse=front_inverse, coupling=coupling, stiffness=stiffness, displacement=displacement, forcing=forcing, lumped_mass=lumped_mass, damping=damping)


def one_substructure(packed):
    inverse_k, masked_k, own_k, stiff_k, live_k = packed
    modes_k = jnp.dot(inverse_k, masked_k, preferred_element_type=jnp.float32).astype(jnp.bfloat16)
    inner = -jnp.dot(own_k, modes_k.T, preferred_element_type=jnp.float32)
    inner = jnp.where(live_k[None, :], inner, jnp.float32(0.0)).astype(jnp.bfloat16)
    contrib_k = jnp.dot(inner, masked_k, preferred_element_type=jnp.float32)
    contrib_k = contrib_k + jnp.dot(own_k, stiff_k, preferred_element_type=jnp.float32)
    return inner, contrib_k, modes_k


def reference(lengths, owners, front_inverse, coupling, stiffness, displacement, forcing, lumped_mass, damping):
    live_rows = jnp.arange(F, dtype=jnp.int32)[None, :] < lengths[:, None]
    masked = jnp.where(live_rows[:, :, None], coupling, jnp.zeros_like(coupling))
    own_disp = displacement[owners[:, 0]]
    interior, contrib, modes = lax.map(one_substructure, (front_inverse, masked, own_disp, stiffness, live_rows))
    gathered = jax.ops.segment_sum(contrib, owners[:, 0], num_segments=NOWN)
    rows = jnp.arange(2 * H, dtype=jnp.int32)
    pair = (rows // 2).astype(jnp.float32)
    parity = (rows % 2).astype(jnp.float32)
    freq = 1.5 * (pair + 1.0) / H
    sign = 1.0 - 2.0 * parity
    disp = displacement.astype(jnp.float32)
    partner = disp.reshape(NOWN, H, 2, NB)[:, :, ::-1, :].reshape(NOWN, 2 * H, NB)
    residual = (gathered
                - (freq * freq)[None, :, None] * lumped_mass[:, None, :] * disp
                + (sign * freq)[None, :, None] * damping[:, None, :] * partner
                - forcing)
    return interior, residual, modes
```

```python
import jax
import jax.numpy as jnp
from jax import lax
from jax.sharding import PartitionSpec as P


def shifted(x, axis, step):
    n = lax.axis_size(axis)
    return lax.ppermute(x, axis, [(j, (j + step) % n) for j in range(n)])


def column_block(x, index, width):
    return lax.dynamic_slice_in_dim(x, index * width, width, axis=x.ndim - 1)


def body(
    lengths, owners, front_inverse, coupling, stiffness, displacement, forcing, lumped_mass, damping
):
    nharm = lax.axis_size("harm")
    harm_idx = lax.axis_index("harm")
    nsub = lax.axis_size("sub")
    front_q = coupling.shape[1]
    width = coupling.shape[2]
    width_q = stiffness.shape[1]
    rows_q = displacement.shape[1]

    own_rows = harm_idx * front_q + jnp.arange(front_q, dtype=jnp.int32)
    live_rows = own_rows[None, :] < lengths[:, None]
    masked = jnp.where(live_rows[:, :, None], coupling, jnp.zeros_like(coupling))

    from_left = shifted(masked, "harm", 1)
    from_right = shifted(masked, "harm", -1)
    half = front_q // 2
    far = jnp.concatenate(
        [shifted(from_left[:, :half], "harm", 1), shifted(from_right[:, half:], "harm", -1)], axis=1
    )

    def modes_term(block, step):
        cols = column_block(front_inverse, (harm_idx + step) % nharm, front_q)
        return jnp.einsum("sfg,sgn->sfn", cols, block, preferred_element_type=jnp.float32)

    modes = modes_term(masked, 0)
    modes = modes + modes_term(from_left, -1)
    modes = modes + modes_term(from_right, 1)
    modes = (modes + modes_term(far, 2)).astype(jnp.bfloat16)

    disp_rows = displacement[0]
    near_block = shifted(disp_rows, "sub", nsub // 2)
    every_block = lax.all_gather(disp_rows, "sub")
    third_block = lax.dynamic_index_in_dim(every_block, owners[2, 0], 0, keepdims=False)
    picked = jnp.stack([near_block, third_block])
    own_pair = lax.all_gather(picked, "harm", axis=1, tiled=True)
    own_disp = jnp.stack([own_pair[0], own_pair[0], own_pair[1]])

    partial_y = jnp.einsum("shn,sfn->shf", own_disp, masked, preferred_element_type=jnp.float32)
    whole_y = lax.all_gather(partial_y, "harm", axis=2, tiled=True)
    inner = -jnp.einsum(
        "shg,sfg->shf",
        whole_y,
        front_inverse.astype(jnp.float32),
        precision=lax.Precision.HIGHEST,
        preferred_element_type=jnp.float32,
    )
    interior = jnp.where(live_rows[:, None, :], inner, jnp.float32(0.0)).astype(jnp.bfloat16)

    disp_cols = column_block(own_disp, harm_idx, width_q)
    contrib = jnp.einsum("shf,sfn->shn", interior, masked, preferred_element_type=jnp.float32)
    contrib = contrib + jnp.einsum(
        "shj,sjn->shn", disp_cols, stiffness, preferred_element_type=jnp.float32
    )
    pair_sum = jnp.stack([contrib[0] + contrib[1], contrib[2]])
    pair_rows = lax.psum_scatter(pair_sum, "harm", scatter_dimension=1, tiled=True)

    near_sum = shifted(pair_rows[0], "sub", nsub // 2)
    slots = jnp.arange(nsub, dtype=jnp.int32)[:, None, None] == owners[2, 0]
    spread = jnp.where(slots, pair_rows[1][None], jnp.float32(0.0))
    far_sum = lax.psum_scatter(spread, "sub", scatter_dimension=0, tiled=True)
    gathered = (near_sum[None] + far_sum)

    pairs_all = rows_q * nharm // 2
    rows = harm_idx * rows_q + jnp.arange(rows_q, dtype=jnp.int32)
    pair = (rows // 2).astype(jnp.float32)
    parity = (rows % 2).astype(jnp.float32)
    freq = 1.5 * (pair + 1.0) / pairs_all
    sign = 1.0 - 2.0 * parity
    disp = displacement.astype(jnp.float32)
    partner = disp.reshape(1, rows_q // 2, 2, width)[:, :, ::-1, :].reshape(1, rows_q, width)
    residual = (
        gathered
        - (freq * freq)[None, :, None] * lumped_mass[:, None, :] * disp
        + (sign * freq)[None, :, None] * damping[:, None, :] * partner
        - forcing
    )
    return (interior, residual, modes)


def solution(mesh):
    placed = (
        P("sub"),
        P("sub", None),
        P("sub", "harm", None),
        P("sub", "harm", None),
        P("sub", "harm", None),
        P("sub", "harm", None),
        P("sub", "harm", None),
        P("sub", None),
        P("sub", None),
    )
    return jax.shard_map(
        body,
        mesh=mesh,
        in_specs=placed,
        out_specs=(P("sub", None, "harm"), P("sub", "harm", None), P("sub", "harm", None)),
        check_vma=False,
    )
```

```python
import jax
import jax.numpy as jnp
from jax import lax
from jax.sharding import Mesh
from jax.sharding import PartitionSpec as P

SUB = ("sub_0", "sub_1", "sub_2")


def copy_for_each(x, axis):
    length = lax.axis_size(axis)
    return lax.all_to_all(jnp.broadcast_to(x[None], (length, *x.shape)), axis, 0, 0, tiled=True)


def joined_along(tiles, dim):
    tiles = jnp.moveaxis(tiles, 0, dim)
    shape = tiles.shape
    return tiles.reshape(*shape[:dim], shape[dim] * shape[dim + 1], *shape[dim + 2 :])


def whole_of(x, axes, dim):
    far, near = axes
    tiles = copy_for_each(copy_for_each(x, far), near)
    return joined_along(tiles.swapaxes(0, 1).reshape(-1, *x.shape), dim)


def collect(x, axis, dim):
    tiles = copy_for_each(x, axis)
    return joined_along(tiles, dim)


def in_blocks(x, dim, length):
    shape = x.shape
    tiles = x.reshape(*shape[:dim], length, shape[dim] // length, *shape[dim + 1 :])
    return jnp.moveaxis(tiles, dim, 0)


def sent_and_summed(x, axis, dim):
    tiles = in_blocks(x, dim, lax.axis_size(axis))
    arrived = lax.all_to_all(tiles, axis, split_axis=0, concat_axis=0, tiled=True)
    return arrived.astype(jnp.float32).sum(axis=0)


def shifted(x, axis, step):
    n = lax.axis_size(axis)
    return lax.ppermute(x, axis, [(j, (j + step) % n) for j in range(n)])


def ring_whole(x, idx, n):
    from_left = shifted(x, "harm", 1)
    from_right = shifted(x, "harm", -1)
    half = x.shape[1] // 2
    far = jnp.concatenate(
        [shifted(from_left[:, :half], "harm", 1), shifted(from_right[:, half:], "harm", -1)], axis=1
    )
    blocks = jnp.stack([x, from_right, far, from_left])
    order = (jnp.arange(n, dtype=jnp.int32) - idx) % n
    return jnp.concatenate([blocks[order[j]] for j in range(n)], axis=1)


def body(
    lengths, owners, front_inverse, coupling, stiffness, displacement, forcing, lumped_mass, damping
):
    nharm = lax.axis_size("harm")
    harm_idx = lax.axis_index("harm")
    front_q = coupling.shape[1]
    width = coupling.shape[2]
    width_q = stiffness.shape[1]
    nown = lax.axis_size(SUB)
    own_rows = harm_idx * front_q + jnp.arange(front_q, dtype=jnp.int32)
    live_rows = own_rows[None, :] < lengths[:, None]
    masked = jnp.where(live_rows[:, :, None], coupling, jnp.zeros_like(coupling))
    longest = jnp.max(lengths)
    empty = jnp.zeros((masked.shape[0], front_q, width), jnp.float32)
    piece = ring_whole(masked, harm_idx, nharm)
    modes = lax.cond(
        jnp.int32(0) < longest,
        lambda: jnp.einsum(
            "sfg,sgn->sfn", front_inverse, piece, preferred_element_type=jnp.float32
        ),
        lambda: empty,
    ).astype(jnp.bfloat16)
    selector = (owners[:, 0][:, None] == jnp.arange(nown, dtype=jnp.int32)[None, :]).astype(
        jnp.bfloat16
    )
    group = whole_of(displacement, (("sub_0", "sub_1"), "sub_2"), 0)
    picked = jnp.einsum("so,ohn->shn", selector, group, preferred_element_type=jnp.float32).astype(
        jnp.bfloat16
    )
    own_disp = collect(picked, "harm", 1)
    inner = -jnp.einsum("sfn,shn->shf", modes, own_disp, preferred_element_type=jnp.float32)
    interior = jnp.where(live_rows[:, None, :], inner, jnp.float32(0.0)).astype(jnp.bfloat16)
    disp_cols = lax.dynamic_slice_in_dim(own_disp, harm_idx * width_q, width_q, 2)
    contrib = jnp.einsum("shf,sfn->shn", interior, masked, preferred_element_type=jnp.float32)
    contrib = contrib + jnp.einsum(
        "shj,sjn->shn", disp_cols, stiffness, preferred_element_type=jnp.float32
    )
    partial_rows = sent_and_summed(contrib.astype(jnp.bfloat16), "harm", 1)
    routing = (jnp.arange(nown, dtype=jnp.int32)[:, None] == owners[:, 0][None, :]).astype(
        jnp.float32
    )
    dense = jnp.einsum("os,shn->ohn", routing, partial_rows, precision=lax.Precision.HIGHEST)
    arrived = lax.all_to_all(
        dense.astype(jnp.bfloat16), SUB, split_axis=0, concat_axis=0, tiled=True
    ).astype(dense.dtype)
    gathered = jnp.sum(arrived, axis=0, keepdims=True)
    rows_q = displacement.shape[1]
    pairs_all = rows_q * nharm // 2
    rows = harm_idx * rows_q + jnp.arange(rows_q, dtype=jnp.int32)
    pair = (rows // 2).astype(jnp.float32)
    parity = (rows % 2).astype(jnp.float32)
    freq = 1.5 * (pair + 1.0) / pairs_all
    sign = 1.0 - 2.0 * parity
    disp = displacement.astype(jnp.float32)
    partner = disp.reshape(1, rows_q // 2, 2, width)[:, :, ::-1, :].reshape(1, rows_q, width)
    residual = (
        gathered
        - (freq * freq)[None, :, None] * lumped_mass[:, None, :] * disp
        + (sign * freq)[None, :, None] * damping[:, None, :] * partner
        - forcing
    )
    return (interior, residual, modes)


def solution(mesh):
    split = Mesh(
        mesh.devices.reshape(8, 8, 2, mesh.shape["harm"]), ("sub_0", "sub_1", "sub_2", "harm")
    )
    placed = (
        P(SUB),
        P(SUB, None),
        P(SUB, "harm", None),
        P(SUB, "harm", None),
        P(SUB, "harm", None),
        P(SUB, "harm", None),
        P(SUB, "harm", None),
        P(SUB, None),
        P(SUB, None),
    )
    return jax.shard_map(
        body,
        mesh=split,
        in_specs=placed,
        out_specs=(P(SUB, None, "harm"), P(SUB, "harm", None), P(SUB, "harm", None)),
        check_vma=False,
    )
```

```python
import jax
import jax.numpy as jnp
from jax import lax
from jax.sharding import Mesh
from jax.sharding import PartitionSpec as P

SUB = ("sub_0", "sub_1", "sub_2")
PLANE = ("sub_0", "sub_1")


def copy_for_each(x, axis):
    length = lax.axis_size(axis)
    return lax.all_to_all(jnp.broadcast_to(x[None], (length, *x.shape)), axis, 0, 0, tiled=True)


def joined_along(tiles, dim):
    tiles = jnp.moveaxis(tiles, 0, dim)
    shape = tiles.shape
    return tiles.reshape(*shape[:dim], shape[dim] * shape[dim + 1], *shape[dim + 2 :])


def whole_of(x, axes, dim):
    far, near = axes
    tiles = copy_for_each(copy_for_each(x, far), near)
    return joined_along(tiles.swapaxes(0, 1).reshape(-1, *x.shape), dim)


def collect(x, axis, dim):
    tiles = copy_for_each(x, axis)
    return joined_along(tiles, dim)


def in_blocks(x, dim, length):
    shape = x.shape
    tiles = x.reshape(*shape[:dim], length, shape[dim] // length, *shape[dim + 1 :])
    return jnp.moveaxis(tiles, dim, 0)


def sent_and_summed(x, axis, dim):
    tiles = in_blocks(x, dim, lax.axis_size(axis))
    arrived = lax.all_to_all(tiles, axis, split_axis=0, concat_axis=0, tiled=True)
    return arrived.astype(jnp.float32).sum(axis=0)


def body(
    lengths, owners, front_inverse, coupling, stiffness, displacement, forcing, lumped_mass, damping
):
    nharm = lax.axis_size("harm")
    harm_idx = lax.axis_index("harm")
    front_q = coupling.shape[1]
    width = coupling.shape[2]
    width_q = stiffness.shape[1]
    nown = lax.axis_size(SUB)
    own_rows = harm_idx * front_q + jnp.arange(front_q, dtype=jnp.int32)
    live_rows = own_rows[None, :] < lengths[:, None]
    masked = jnp.where(live_rows[:, :, None], coupling, jnp.zeros_like(coupling))
    longest = jnp.max(lengths)
    empty = jnp.zeros((masked.shape[0], front_q, width), jnp.float32)
    piece = lax.all_gather(masked, "harm", axis=1, tiled=True)
    modes = lax.cond(
        jnp.int32(0) < longest,
        lambda: jnp.einsum(
            "sfg,sgn->sfn", front_inverse, piece, preferred_element_type=jnp.float32
        ),
        lambda: empty,
    ).astype(jnp.bfloat16)
    nplane = lax.axis_size(PLANE)
    core = lax.axis_index("sub_2")
    near = (lax.axis_index(SUB) + nown // 2) % nown
    third = owners[2, 0]
    other = lax.ppermute(owners[2:3, 0], "sub_2", [(0, 1), (1, 0)])[0]
    plane = copy_for_each(displacement[0], PLANE)
    lent = lax.ppermute(
        lax.dynamic_index_in_dim(plane, other // 2, 0, keepdims=False), "sub_2", [(0, 1), (1, 0)]
    )
    here = lax.dynamic_index_in_dim(plane, third // 2, 0, keepdims=False)
    picked = jnp.stack(
        [
            lax.dynamic_index_in_dim(plane, near // 2, 0, keepdims=False),
            jnp.where(third % 2 == core, here, lent),
        ]
    )
    own_pair = collect(picked, "harm", 1)
    own_disp = jnp.stack([own_pair[0], own_pair[0], own_pair[1]])
    inner = -jnp.einsum("sfn,shn->shf", modes, own_disp, preferred_element_type=jnp.float32)
    interior = jnp.where(live_rows[:, None, :], inner, jnp.float32(0.0)).astype(jnp.bfloat16)
    disp_cols = lax.dynamic_slice_in_dim(own_disp, harm_idx * width_q, width_q, 2)
    contrib = jnp.einsum("shf,sfn->shn", interior, masked, preferred_element_type=jnp.float32)
    contrib = contrib + jnp.einsum(
        "shj,sjn->shn", disp_cols, stiffness, preferred_element_type=jnp.float32
    )
    partial_rows = sent_and_summed(contrib.astype(jnp.bfloat16), "harm", 1)
    near_part = partial_rows[0] + partial_rows[1]
    third_part = partial_rows[2]
    other_part = lax.ppermute(third_part, "sub_2", [(0, 1), (1, 0)])
    slots = jnp.arange(nplane, dtype=jnp.int32)[:, None, None]
    dense = (
        jnp.where(slots == near // 2, near_part, jnp.float32(0.0))
        + jnp.where((slots == third // 2) & (third % 2 == core), third_part, jnp.float32(0.0))
        + jnp.where((slots == other // 2) & (other % 2 == core), other_part, jnp.float32(0.0))
    )
    arrived = lax.all_to_all(
        dense.astype(jnp.bfloat16), PLANE, split_axis=0, concat_axis=0, tiled=True
    ).astype(jnp.float32)
    gathered = jnp.sum(arrived, axis=0, keepdims=True)
    rows_q = displacement.shape[1]
    pairs_all = rows_q * nharm // 2
    rows = harm_idx * rows_q + jnp.arange(rows_q, dtype=jnp.int32)
    pair = (rows // 2).astype(jnp.float32)
    parity = (rows % 2).astype(jnp.float32)
    freq = 1.5 * (pair + 1.0) / pairs_all
    sign = 1.0 - 2.0 * parity
    disp = displacement.astype(jnp.float32)
    partner = disp.reshape(1, rows_q // 2, 2, width)[:, :, ::-1, :].reshape(1, rows_q, width)
    residual = (
        gathered
        - (freq * freq)[None, :, None] * lumped_mass[:, None, :] * disp
        + (sign * freq)[None, :, None] * damping[:, None, :] * partner
        - forcing
    )
    return (interior, residual, modes)


def solution(mesh):
    split = Mesh(
        mesh.devices.reshape(8, 8, 2, mesh.shape["harm"]), ("sub_0", "sub_1", "sub_2", "harm")
    )
    placed = (
        P(SUB),
        P(SUB, None),
        P(SUB, "harm", None),
        P(SUB, "harm", None),
        P(SUB, "harm", None),
        P(SUB, "harm", None),
        P(SUB, "harm", None),
        P(SUB, None),
        P(SUB, None),
    )
    return jax.shard_map(
        body,
        mesh=split,
        in_specs=placed,
        out_specs=(P(SUB, None, "harm"), P(SUB, "harm", None), P(SUB, "harm", None)),
        check_vma=False,
    )
```

```python
import jax
import jax.numpy as jnp
from jax import lax
from jax.sharding import Mesh
from jax.sharding import PartitionSpec as P

SUB = ("sub_0", "sub_1", "sub_2")
PLANE = ("sub_0", "sub_1")
PAIR = ("sub_2", "harm")


def copy_for_each(x, axis):
    length = lax.axis_size(axis)
    return lax.all_to_all(jnp.broadcast_to(x[None], (length, *x.shape)), axis, 0, 0, tiled=True)


def joined_along(tiles, dim):
    tiles = jnp.moveaxis(tiles, 0, dim)
    shape = tiles.shape
    return tiles.reshape(*shape[:dim], shape[dim] * shape[dim + 1], *shape[dim + 2 :])


def whole_of(x, axes, dim):
    far, near = axes
    tiles = copy_for_each(copy_for_each(x, far), near)
    return joined_along(tiles.swapaxes(0, 1).reshape(-1, *x.shape), dim)


def collect(x, axis, dim):
    tiles = copy_for_each(x, axis)
    return joined_along(tiles, dim)


def in_blocks(x, dim, length):
    shape = x.shape
    tiles = x.reshape(*shape[:dim], length, shape[dim] // length, *shape[dim + 1 :])
    return jnp.moveaxis(tiles, dim, 0)


def sent_and_summed(x, axis, dim):
    tiles = in_blocks(x, dim, lax.axis_size(axis))
    arrived = lax.all_to_all(tiles, axis, split_axis=0, concat_axis=0, tiled=True)
    return arrived.astype(jnp.float32).sum(axis=0)


def body(
    lengths, owners, front_inverse, coupling, stiffness, displacement, forcing, lumped_mass, damping
):
    nharm = lax.axis_size("harm")
    harm_idx = lax.axis_index("harm")
    front_q = coupling.shape[1]
    width = coupling.shape[2]
    width_q = stiffness.shape[1]
    nown = lax.axis_size(SUB)
    own_rows = harm_idx * front_q + jnp.arange(front_q, dtype=jnp.int32)
    live_rows = own_rows[None, :] < lengths[:, None]
    masked = jnp.where(live_rows[:, :, None], coupling, jnp.zeros_like(coupling))
    longest = jnp.max(lengths)
    empty = jnp.zeros((masked.shape[0], front_q, width), jnp.float32)
    whole_live = jnp.arange(nharm * front_q, dtype=jnp.int32)[None, :] < lengths[:, None]
    piece = lax.all_gather(coupling, "harm", axis=1, tiled=True)
    piece = jnp.where(whole_live[:, :, None], piece, jnp.zeros_like(piece))
    modes = lax.cond(
        jnp.int32(0) < longest,
        lambda: jnp.einsum(
            "sfg,sgn->sfn", front_inverse, piece, preferred_element_type=jnp.float32
        ),
        lambda: empty,
    ).astype(jnp.bfloat16)
    nplane = lax.axis_size(PLANE)
    rows_q = displacement.shape[1]
    core = lax.axis_index("sub_2")
    near = (lax.axis_index(SUB) + nown // 2) % nown
    third = owners[2, 0]
    other = lax.ppermute(owners[2:3, 0], "sub_2", [(0, 1), (1, 0)])[0]
    plane = copy_for_each(displacement[0], PLANE)
    zero_block = jnp.zeros_like(plane[0])
    lend = []
    for peer_core in range(2):
        wanted = jnp.where(peer_core == core, third, other)
        lend.append(
            jnp.stack(
                [
                    jnp.where(
                        peer_core == core,
                        lax.dynamic_index_in_dim(plane, near // 2, 0, keepdims=False),
                        zero_block,
                    ),
                    jnp.where(
                        wanted % 2 == core,
                        lax.dynamic_index_in_dim(plane, wanted // 2, 0, keepdims=False),
                        zero_block,
                    ),
                ]
            )
        )
    lend = jnp.broadcast_to(jnp.stack(lend)[:, None], (2, nharm, 2, *zero_block.shape))
    lent = lax.all_to_all(
        lend.reshape(2 * nharm, 2, *zero_block.shape), PAIR, 0, 0, tiled=True
    ).reshape(2, nharm, 2, *zero_block.shape)
    lent = (lent[0] + lent[1]).transpose(1, 0, 2, 3)
    own_pair = lent.reshape(2, nharm * zero_block.shape[0], width)
    own_disp = jnp.stack([own_pair[0], own_pair[0], own_pair[1]])
    inner = -jnp.einsum("sfn,shn->shf", modes, own_disp, preferred_element_type=jnp.float32)
    interior = jnp.where(live_rows[:, None, :], inner, jnp.float32(0.0)).astype(jnp.bfloat16)
    disp_cols = lax.dynamic_slice_in_dim(own_disp, harm_idx * width_q, width_q, 2)
    contrib = jnp.einsum("shf,sfn->shn", interior, masked, preferred_element_type=jnp.float32)
    contrib = contrib + jnp.einsum(
        "shj,sjn->shn", disp_cols, stiffness, preferred_element_type=jnp.float32
    )
    near_c = (contrib[0] + contrib[1]).reshape(nharm, rows_q, width)
    third_c = contrib[2].reshape(nharm, rows_q, width)
    zero_rows = jnp.zeros_like(near_c)
    send = jnp.stack(
        [
            jnp.stack(
                [
                    jnp.where(peer_core == core, near_c, zero_rows),
                    jnp.where(third % 2 == peer_core, third_c, zero_rows),
                ],
                axis=1,
            )
            for peer_core in range(2)
        ]
    )
    came = lax.all_to_all(
        send.reshape(2 * nharm, 2, rows_q, width).astype(jnp.bfloat16), PAIR, 0, 0, tiled=True
    ).astype(jnp.float32)
    came = came.reshape(2, nharm, 2, rows_q, width).sum(axis=1)
    mine = jnp.where(core == 0, came[0], came[1])
    theirs = jnp.where(core == 0, came[1], came[0])
    near_part = mine[0]
    third_part = mine[1]
    other_part = theirs[1]
    slots = jnp.arange(nplane, dtype=jnp.int32)[:, None, None]
    dense = (
        jnp.where(slots == near // 2, near_part, jnp.float32(0.0))
        + jnp.where((slots == third // 2) & (third % 2 == core), third_part, jnp.float32(0.0))
        + jnp.where((slots == other // 2) & (other % 2 == core), other_part, jnp.float32(0.0))
    )
    arrived = lax.all_to_all(
        dense.astype(jnp.bfloat16), PLANE, split_axis=0, concat_axis=0, tiled=True
    ).astype(jnp.float32)
    gathered = jnp.sum(arrived, axis=0, keepdims=True)
    rows_q = displacement.shape[1]
    pairs_all = rows_q * nharm // 2
    rows = harm_idx * rows_q + jnp.arange(rows_q, dtype=jnp.int32)
    pair = (rows // 2).astype(jnp.float32)
    parity = (rows % 2).astype(jnp.float32)
    freq = 1.5 * (pair + 1.0) / pairs_all
    sign = 1.0 - 2.0 * parity
    disp = displacement.astype(jnp.float32)
    partner = disp.reshape(1, rows_q // 2, 2, width)[:, :, ::-1, :].reshape(1, rows_q, width)
    residual = (
        gathered
        - (freq * freq)[None, :, None] * lumped_mass[:, None, :] * disp
        + (sign * freq)[None, :, None] * damping[:, None, :] * partner
        - forcing
    )
    return (interior, residual, modes)


def solution(mesh):
    split = Mesh(
        mesh.devices.reshape(8, 8, 2, mesh.shape["harm"]), ("sub_0", "sub_1", "sub_2", "harm")
    )
    placed = (
        P(SUB),
        P(SUB, None),
        P(SUB, "harm", None),
        P(SUB, "harm", None),
        P(SUB, "harm", None),
        P(SUB, "harm", None),
        P(SUB, "harm", None),
        P(SUB, None),
        P(SUB, None),
    )
    return jax.shard_map(
        body,
        mesh=split,
        in_specs=placed,
        out_specs=(P(SUB, None, "harm"), P(SUB, "harm", None), P(SUB, "harm", None)),
        check_vma=False,
    )
```

```python
import jax
import jax.numpy as jnp
from jax import lax
from jax.sharding import Mesh
from jax.sharding import PartitionSpec as P

SUB = ("sub_0", "sub_1", "sub_2")
PLANE = ("sub_0", "sub_1")
PAIR = ("sub_2", "harm")


def copy_for_each(x, axis):
    length = lax.axis_size(axis)
    return lax.all_to_all(jnp.broadcast_to(x[None], (length, *x.shape)), axis, 0, 0, tiled=True)


def joined_along(tiles, dim):
    tiles = jnp.moveaxis(tiles, 0, dim)
    shape = tiles.shape
    return tiles.reshape(*shape[:dim], shape[dim] * shape[dim + 1], *shape[dim + 2 :])


def whole_of(x, axes, dim):
    far, near = axes
    tiles = copy_for_each(copy_for_each(x, far), near)
    return joined_along(tiles.swapaxes(0, 1).reshape(-1, *x.shape), dim)


def collect(x, axis, dim):
    tiles = copy_for_each(x, axis)
    return joined_along(tiles, dim)


def in_blocks(x, dim, length):
    shape = x.shape
    tiles = x.reshape(*shape[:dim], length, shape[dim] // length, *shape[dim + 1 :])
    return jnp.moveaxis(tiles, dim, 0)


def sent_and_summed(x, axis, dim):
    tiles = in_blocks(x, dim, lax.axis_size(axis))
    arrived = lax.all_to_all(tiles, axis, split_axis=0, concat_axis=0, tiled=True)
    return arrived.astype(jnp.float32).sum(axis=0)


def body(
    lengths, owners, front_inverse, coupling, stiffness, displacement, forcing, lumped_mass, damping
):
    nharm = lax.axis_size("harm")
    harm_idx = lax.axis_index("harm")
    front_q = coupling.shape[1]
    width = coupling.shape[2]
    width_q = stiffness.shape[1]
    nown = lax.axis_size(SUB)
    own_rows = harm_idx * front_q + jnp.arange(front_q, dtype=jnp.int32)
    live_rows = own_rows[None, :] < lengths[:, None]
    masked = jnp.where(live_rows[:, :, None], coupling, jnp.zeros_like(coupling))
    whole_live = jnp.arange(nharm * front_q, dtype=jnp.int32)[None, :] < lengths[:, None]
    piece = lax.all_gather(coupling, "harm", axis=1, tiled=True)
    piece = jnp.where(whole_live[:, :, None], piece, jnp.zeros_like(piece))
    modes = jnp.einsum(
        "sfg,sgn->sfn", front_inverse, piece, preferred_element_type=jnp.float32
    ).astype(jnp.bfloat16)
    nplane = lax.axis_size(PLANE)
    rows_q = displacement.shape[1]
    core = lax.axis_index("sub_2")
    near = (lax.axis_index(SUB) + nown // 2) % nown
    third = owners[2, 0]
    other = lax.ppermute(owners[2:3, 0], "sub_2", [(0, 1), (1, 0)])[0]
    plane = copy_for_each(displacement[0], PLANE)
    zero_block = jnp.zeros_like(plane[0])
    lend = []
    for peer_core in range(2):
        wanted = jnp.where(peer_core == core, third, other)
        lend.append(
            jnp.stack(
                [
                    jnp.where(
                        peer_core == core,
                        lax.dynamic_index_in_dim(plane, near // 2, 0, keepdims=False),
                        zero_block,
                    ),
                    jnp.where(
                        wanted % 2 == core,
                        lax.dynamic_index_in_dim(plane, wanted // 2, 0, keepdims=False),
                        zero_block,
                    ),
                ]
            )
        )
    lend = jnp.broadcast_to(jnp.stack(lend)[:, None], (2, nharm, 2, *zero_block.shape))
    lent = lax.all_to_all(
        lend.reshape(2 * nharm, 2, *zero_block.shape), PAIR, 0, 0, tiled=True
    ).reshape(2, nharm, 2, *zero_block.shape)
    lent = (lent[0] + lent[1]).transpose(1, 0, 2, 3)
    own_pair = lent.reshape(2, nharm * zero_block.shape[0], width)
    own_disp = jnp.stack([own_pair[0], own_pair[0], own_pair[1]])
    partial_y = jnp.einsum("shn,sfn->shf", own_disp, masked, preferred_element_type=jnp.float32)
    whole_y = collect(partial_y, "harm", 2)
    inner = -jnp.einsum(
        "shg,sfg->shf",
        whole_y,
        front_inverse.astype(jnp.float32),
        precision=lax.Precision.HIGHEST,
        preferred_element_type=jnp.float32,
    )
    interior = jnp.where(live_rows[:, None, :], inner, jnp.float32(0.0)).astype(jnp.bfloat16)
    disp_cols = lax.dynamic_slice_in_dim(own_disp, harm_idx * width_q, width_q, 2)
    contrib = jnp.einsum("shf,sfn->shn", interior, masked, preferred_element_type=jnp.float32)
    contrib = contrib + jnp.einsum(
        "shj,sjn->shn", disp_cols, stiffness, preferred_element_type=jnp.float32
    )
    near_c = (contrib[0] + contrib[1]).reshape(nharm, rows_q, width)
    third_c = contrib[2].reshape(nharm, rows_q, width)
    zero_rows = jnp.zeros_like(near_c)
    send = jnp.stack(
        [
            jnp.stack(
                [
                    jnp.where(peer_core == core, near_c, zero_rows),
                    jnp.where(third % 2 == peer_core, third_c, zero_rows),
                ],
                axis=1,
            )
            for peer_core in range(2)
        ]
    )
    came = lax.all_to_all(
        send.reshape(2 * nharm, 2, rows_q, width).astype(jnp.bfloat16), PAIR, 0, 0, tiled=True
    ).astype(jnp.float32)
    came = came.reshape(2, nharm, 2, rows_q, width).sum(axis=1)
    mine = jnp.where(core == 0, came[0], came[1])
    theirs = jnp.where(core == 0, came[1], came[0])
    near_part = mine[0]
    third_part = mine[1]
    other_part = theirs[1]
    slots = jnp.arange(nplane, dtype=jnp.int32)[:, None, None]
    dense = (
        jnp.where(slots == near // 2, near_part, jnp.float32(0.0))
        + jnp.where((slots == third // 2) & (third % 2 == core), third_part, jnp.float32(0.0))
        + jnp.where((slots == other // 2) & (other % 2 == core), other_part, jnp.float32(0.0))
    )
    arrived = lax.all_to_all(
        dense.astype(jnp.bfloat16), PLANE, split_axis=0, concat_axis=0, tiled=True
    ).astype(jnp.float32)
    gathered = jnp.sum(arrived, axis=0, keepdims=True)
    rows_q = displacement.shape[1]
    pairs_all = rows_q * nharm // 2
    rows = harm_idx * rows_q + jnp.arange(rows_q, dtype=jnp.int32)
    pair = (rows // 2).astype(jnp.float32)
    parity = (rows % 2).astype(jnp.float32)
    freq = 1.5 * (pair + 1.0) / pairs_all
    sign = 1.0 - 2.0 * parity
    disp = displacement.astype(jnp.float32)
    partner = disp.reshape(1, rows_q // 2, 2, width)[:, :, ::-1, :].reshape(1, rows_q, width)
    residual = (
        gathered
        - (freq * freq)[None, :, None] * lumped_mass[:, None, :] * disp
        + (sign * freq)[None, :, None] * damping[:, None, :] * partner
        - forcing
    )
    return (interior, residual, modes)


def solution(mesh):
    split = Mesh(
        mesh.devices.reshape(8, 8, 2, mesh.shape["harm"]), ("sub_0", "sub_1", "sub_2", "harm")
    )
    placed = (
        P(SUB),
        P(SUB, None),
        P(SUB, "harm", None),
        P(SUB, "harm", None),
        P(SUB, "harm", None),
        P(SUB, "harm", None),
        P(SUB, "harm", None),
        P(SUB, None),
        P(SUB, None),
    )
    return jax.shard_map(
        body,
        mesh=split,
        in_specs=placed,
        out_specs=(P(SUB, None, "harm"), P(SUB, "harm", None), P(SUB, "harm", None)),
        check_vma=False,
    )
```

```python
import jax
import jax.numpy as jnp
from jax import lax
from jax.sharding import Mesh
from jax.sharding import PartitionSpec as P

SUB = ("sub_0", "sub_1", "sub_2")
PLANE = ("sub_0", "sub_1")
PAIR = ("sub_2", "harm")


def copy_for_each(x, axis):
    length = lax.axis_size(axis)
    return lax.all_to_all(jnp.broadcast_to(x[None], (length, *x.shape)), axis, 0, 0, tiled=True)


def joined_along(tiles, dim):
    tiles = jnp.moveaxis(tiles, 0, dim)
    shape = tiles.shape
    return tiles.reshape(*shape[:dim], shape[dim] * shape[dim + 1], *shape[dim + 2 :])


def whole_of(x, axes, dim):
    far, near = axes
    tiles = copy_for_each(copy_for_each(x, far), near)
    return joined_along(tiles.swapaxes(0, 1).reshape(-1, *x.shape), dim)


def collect(x, axis, dim):
    tiles = copy_for_each(x, axis)
    return joined_along(tiles, dim)


def in_blocks(x, dim, length):
    shape = x.shape
    tiles = x.reshape(*shape[:dim], length, shape[dim] // length, *shape[dim + 1 :])
    return jnp.moveaxis(tiles, dim, 0)


def sent_and_summed(x, axis, dim):
    tiles = in_blocks(x, dim, lax.axis_size(axis))
    arrived = lax.all_to_all(tiles, axis, split_axis=0, concat_axis=0, tiled=True)
    return arrived.astype(jnp.float32).sum(axis=0)


def shifted(x, axis, step):
    n = lax.axis_size(axis)
    return lax.ppermute(x, axis, [(j, (j + step) % n) for j in range(n)])


def ring_whole(x, idx, n):
    from_left = shifted(x, "harm", 1)
    from_right = shifted(x, "harm", -1)
    half = x.shape[1] // 2
    far = jnp.concatenate(
        [shifted(from_left[:, :half], "harm", 1), shifted(from_right[:, half:], "harm", -1)], axis=1
    )
    blocks = jnp.stack([x, from_right, far, from_left])
    order = (jnp.arange(n, dtype=jnp.int32) - idx) % n
    return jnp.concatenate([blocks[order[j]] for j in range(n)], axis=1)


def body(
    lengths, owners, front_inverse, coupling, stiffness, displacement, forcing, lumped_mass, damping
):
    nharm = lax.axis_size("harm")
    harm_idx = lax.axis_index("harm")
    front_q = coupling.shape[1]
    width = coupling.shape[2]
    width_q = stiffness.shape[1]
    nown = lax.axis_size(SUB)
    own_rows = harm_idx * front_q + jnp.arange(front_q, dtype=jnp.int32)
    live_rows = own_rows[None, :] < lengths[:, None]
    masked = jnp.where(live_rows[:, :, None], coupling, jnp.zeros_like(coupling))
    nplane = lax.axis_size(PLANE)
    rows_q = displacement.shape[1]
    core = lax.axis_index("sub_2")
    near = (lax.axis_index(SUB) + nown // 2) % nown
    third = owners[2, 0]
    other = lax.ppermute(owners[2:3, 0], "sub_2", [(0, 1), (1, 0)])[0]
    plane = copy_for_each(displacement[0], PLANE)
    zero_block = jnp.zeros_like(plane[0])
    anchor = plane[0, 0, 0] * jnp.zeros((), plane.dtype)
    piece = ring_whole(masked + anchor, harm_idx, nharm)
    modes = jnp.einsum(
        "sfg,sgn->sfn", front_inverse, piece, preferred_element_type=jnp.float32
    ).astype(jnp.bfloat16)
    lend = []
    for peer_core in range(2):
        wanted = jnp.where(peer_core == core, third, other)
        lend.append(
            jnp.stack(
                [
                    jnp.where(
                        peer_core == core,
                        lax.dynamic_index_in_dim(plane, near // 2, 0, keepdims=False),
                        zero_block,
                    ),
                    jnp.where(
                        wanted % 2 == core,
                        lax.dynamic_index_in_dim(plane, wanted // 2, 0, keepdims=False),
                        zero_block,
                    ),
                ]
            )
        )
    lend = jnp.broadcast_to(jnp.stack(lend)[:, None], (2, nharm, 2, *zero_block.shape))
    lent = lax.all_to_all(
        lend.reshape(2 * nharm, 2, *zero_block.shape), PAIR, 0, 0, tiled=True
    ).reshape(2, nharm, 2, *zero_block.shape)
    lent = (lent[0] + lent[1]).transpose(1, 0, 2, 3)
    own_pair = lent.reshape(2, nharm * zero_block.shape[0], width)
    own_disp = jnp.stack([own_pair[0], own_pair[0], own_pair[1]])
    partial_y = jnp.einsum("shn,sfn->shf", own_disp, masked, preferred_element_type=jnp.float32)
    whole_y = collect(partial_y, "harm", 2)
    inner = -jnp.einsum(
        "shg,sfg->shf",
        whole_y,
        front_inverse.astype(jnp.float32),
        precision=lax.Precision.HIGHEST,
        preferred_element_type=jnp.float32,
    )
    interior = jnp.where(live_rows[:, None, :], inner, jnp.float32(0.0)).astype(jnp.bfloat16)
    disp_cols = lax.dynamic_slice_in_dim(own_disp, harm_idx * width_q, width_q, 2)
    contrib = jnp.einsum("shf,sfn->shn", interior, masked, preferred_element_type=jnp.float32)
    contrib = contrib + jnp.einsum(
        "shj,sjn->shn", disp_cols, stiffness, preferred_element_type=jnp.float32
    )
    near_c = (contrib[0] + contrib[1]).reshape(nharm, rows_q, width)
    third_c = contrib[2].reshape(nharm, rows_q, width)
    zero_rows = jnp.zeros_like(near_c)
    send = jnp.stack(
        [
            jnp.stack(
                [
                    jnp.where(peer_core == core, near_c, zero_rows),
                    jnp.where(third % 2 == peer_core, third_c, zero_rows),
                ],
                axis=1,
            )
            for peer_core in range(2)
        ]
    )
    came = lax.all_to_all(
        send.reshape(2 * nharm, 2, rows_q, width).astype(jnp.bfloat16), PAIR, 0, 0, tiled=True
    ).astype(jnp.float32)
    came = came.reshape(2, nharm, 2, rows_q, width).sum(axis=1)
    mine = jnp.where(core == 0, came[0], came[1])
    theirs = jnp.where(core == 0, came[1], came[0])
    near_part = mine[0]
    third_part = mine[1]
    other_part = theirs[1]
    slots = jnp.arange(nplane, dtype=jnp.int32)[:, None, None]
    dense = (
        jnp.where(slots == near // 2, near_part, jnp.float32(0.0))
        + jnp.where((slots == third // 2) & (third % 2 == core), third_part, jnp.float32(0.0))
        + jnp.where((slots == other // 2) & (other % 2 == core), other_part, jnp.float32(0.0))
    )
    arrived = lax.all_to_all(
        dense.astype(jnp.bfloat16), PLANE, split_axis=0, concat_axis=0, tiled=True
    ).astype(jnp.float32)
    gathered = jnp.sum(arrived, axis=0, keepdims=True)
    rows_q = displacement.shape[1]
    pairs_all = rows_q * nharm // 2
    rows = harm_idx * rows_q + jnp.arange(rows_q, dtype=jnp.int32)
    pair = (rows // 2).astype(jnp.float32)
    parity = (rows % 2).astype(jnp.float32)
    freq = 1.5 * (pair + 1.0) / pairs_all
    sign = 1.0 - 2.0 * parity
    disp = displacement.astype(jnp.float32)
    partner = disp.reshape(1, rows_q // 2, 2, width)[:, :, ::-1, :].reshape(1, rows_q, width)
    residual = (
        gathered
        - (freq * freq)[None, :, None] * lumped_mass[:, None, :] * disp
        + (sign * freq)[None, :, None] * damping[:, None, :] * partner
        - forcing
    )
    return (interior, residual, modes)


def solution(mesh):
    split = Mesh(
        mesh.devices.reshape(8, 8, 2, mesh.shape["harm"]), ("sub_0", "sub_1", "sub_2", "harm")
    )
    placed = (
        P(SUB),
        P(SUB, None),
        P(SUB, "harm", None),
        P(SUB, "harm", None),
        P(SUB, "harm", None),
        P(SUB, "harm", None),
        P(SUB, "harm", None),
        P(SUB, None),
        P(SUB, None),
    )
    return jax.shard_map(
        body,
        mesh=split,
        in_specs=placed,
        out_specs=(P(SUB, None, "harm"), P(SUB, "harm", None), P(SUB, "harm", None)),
        check_vma=False,
    )
```

```python
import jax
import jax.numpy as jnp
from jax import lax
from jax.sharding import Mesh
from jax.sharding import PartitionSpec as P

SUB = ("sub_0", "sub_1", "sub_2")
PLANE = ("sub_0", "sub_1")
PAIR = ("sub_2", "harm")


def copy_for_each(x, axis):
    length = lax.axis_size(axis)
    return lax.all_to_all(jnp.broadcast_to(x[None], (length, *x.shape)), axis, 0, 0, tiled=True)


def joined_along(tiles, dim):
    tiles = jnp.moveaxis(tiles, 0, dim)
    shape = tiles.shape
    return tiles.reshape(*shape[:dim], shape[dim] * shape[dim + 1], *shape[dim + 2 :])


def whole_of(x, axes, dim):
    far, near = axes
    tiles = copy_for_each(copy_for_each(x, far), near)
    return joined_along(tiles.swapaxes(0, 1).reshape(-1, *x.shape), dim)


def collect(x, axis, dim):
    tiles = copy_for_each(x, axis)
    return joined_along(tiles, dim)


def in_blocks(x, dim, length):
    shape = x.shape
    tiles = x.reshape(*shape[:dim], length, shape[dim] // length, *shape[dim + 1 :])
    return jnp.moveaxis(tiles, dim, 0)


def sent_and_summed(x, axis, dim):
    tiles = in_blocks(x, dim, lax.axis_size(axis))
    arrived = lax.all_to_all(tiles, axis, split_axis=0, concat_axis=0, tiled=True)
    return arrived.astype(jnp.float32).sum(axis=0)


def body(
    lengths, owners, front_inverse, coupling, stiffness, displacement, forcing, lumped_mass, damping
):
    nharm = lax.axis_size("harm")
    harm_idx = lax.axis_index("harm")
    front_q = coupling.shape[1]
    width = coupling.shape[2]
    width_q = stiffness.shape[1]
    nown = lax.axis_size(SUB)
    own_rows = harm_idx * front_q + jnp.arange(front_q, dtype=jnp.int32)
    live_rows = own_rows[None, :] < lengths[:, None]
    masked = jnp.where(live_rows[:, :, None], coupling, jnp.zeros_like(coupling))
    whole_live = jnp.arange(nharm * front_q, dtype=jnp.int32)[None, :] < lengths[:, None]
    piece = lax.all_gather(coupling, "harm", axis=1, tiled=True)
    piece = jnp.where(whole_live[:, :, None], piece, jnp.zeros_like(piece))
    modes = jnp.einsum(
        "sfg,sgn->sfn", front_inverse, piece, preferred_element_type=jnp.float32
    ).astype(jnp.bfloat16)
    nplane = lax.axis_size(PLANE)
    rows_q = displacement.shape[1]
    core = lax.axis_index("sub_2")
    near = (lax.axis_index(SUB) + nown // 2) % nown
    third = owners[2, 0]
    other = lax.ppermute(owners[2:3, 0], "sub_2", [(0, 1), (1, 0)])[0]
    plane = copy_for_each(displacement[0], PLANE)
    zero_block = jnp.zeros_like(plane[0])
    lend = []
    for peer_core in range(2):
        wanted = jnp.where(peer_core == core, third, other)
        lend.append(
            jnp.stack(
                [
                    jnp.where(
                        peer_core == core,
                        lax.dynamic_index_in_dim(plane, near // 2, 0, keepdims=False),
                        zero_block,
                    ),
                    jnp.where(
                        wanted % 2 == core,
                        lax.dynamic_index_in_dim(plane, wanted // 2, 0, keepdims=False),
                        zero_block,
                    ),
                ]
            )
        )
    lend = jnp.broadcast_to(jnp.stack(lend)[:, None], (2, nharm, 2, *zero_block.shape))
    lent = lax.all_to_all(
        lend.reshape(2 * nharm, 2, *zero_block.shape), PAIR, 0, 0, tiled=True
    ).reshape(2, nharm, 2, *zero_block.shape)
    lent = (lent[0] + lent[1]).transpose(1, 0, 2, 3)
    own_pair = lent.reshape(2, nharm * zero_block.shape[0], width)
    own_disp = jnp.stack([own_pair[0], own_pair[0], own_pair[1]])
    partial_y = jnp.einsum("shn,sfn->shf", own_disp, masked, preferred_element_type=jnp.float32)
    whole_y = collect(partial_y, "harm", 2)
    inner = -jnp.einsum(
        "shg,sfg->shf",
        whole_y,
        front_inverse.astype(jnp.float32),
        precision=lax.Precision.HIGHEST,
        preferred_element_type=jnp.float32,
    )
    interior = jnp.where(live_rows[:, None, :], inner, jnp.float32(0.0)).astype(jnp.bfloat16)
    disp_cols = lax.dynamic_slice_in_dim(own_disp, harm_idx * width_q, width_q, 2)
    contrib = jnp.einsum("shf,sfn->shn", interior, masked, preferred_element_type=jnp.float32)
    contrib = contrib + jnp.einsum(
        "shj,sjn->shn", disp_cols, stiffness, preferred_element_type=jnp.float32
    )
    near_c = (contrib[0] + contrib[1]).reshape(nharm, rows_q, width)
    third_c = contrib[2].reshape(nharm, rows_q, width)
    zero_rows = jnp.zeros_like(near_c)
    send = jnp.stack(
        [
            jnp.stack(
                [
                    jnp.where(peer_core == core, near_c, zero_rows),
                    jnp.where(third % 2 == peer_core, third_c, zero_rows),
                ],
                axis=1,
            )
            for peer_core in range(2)
        ]
    )
    came = lax.all_to_all(
        send.reshape(2 * nharm, 2, rows_q, width).astype(jnp.bfloat16), PAIR, 0, 0, tiled=True
    ).astype(jnp.float32)
    came = came.reshape(2, nharm, 2, rows_q, width).sum(axis=1)
    mine = jnp.where(core == 0, came[0], came[1])
    theirs = jnp.where(core == 0, came[1], came[0])
    near_part = mine[0]
    third_part = mine[1]
    other_part = theirs[1]
    slots = jnp.arange(nplane, dtype=jnp.int32)[:, None, None]
    dense = (
        jnp.where(slots == near // 2, near_part, jnp.float32(0.0))
        + jnp.where((slots == third // 2) & (third % 2 == core), third_part, jnp.float32(0.0))
        + jnp.where((slots == other // 2) & (other % 2 == core), other_part, jnp.float32(0.0))
    )
    dense = dense + piece[0, 0, 0].astype(jnp.float32) * jnp.float32(0.0)
    arrived = lax.all_to_all(
        dense.astype(jnp.bfloat16), PLANE, split_axis=0, concat_axis=0, tiled=True
    ).astype(jnp.float32)
    gathered = jnp.sum(arrived, axis=0, keepdims=True)
    rows_q = displacement.shape[1]
    pairs_all = rows_q * nharm // 2
    rows = harm_idx * rows_q + jnp.arange(rows_q, dtype=jnp.int32)
    pair = (rows // 2).astype(jnp.float32)
    parity = (rows % 2).astype(jnp.float32)
    freq = 1.5 * (pair + 1.0) / pairs_all
    sign = 1.0 - 2.0 * parity
    disp = displacement.astype(jnp.float32)
    partner = disp.reshape(1, rows_q // 2, 2, width)[:, :, ::-1, :].reshape(1, rows_q, width)
    residual = (
        gathered
        - (freq * freq)[None, :, None] * lumped_mass[:, None, :] * disp
        + (sign * freq)[None, :, None] * damping[:, None, :] * partner
        - forcing
    )
    return (interior, residual, modes)


def solution(mesh):
    split = Mesh(
        mesh.devices.reshape(8, 8, 2, mesh.shape["harm"]), ("sub_0", "sub_1", "sub_2", "harm")
    )
    placed = (
        P(SUB),
        P(SUB, None),
        P(SUB, "harm", None),
        P(SUB, "harm", None),
        P(SUB, "harm", None),
        P(SUB, "harm", None),
        P(SUB, "harm", None),
        P(SUB, None),
        P(SUB, None),
    )
    return jax.shard_map(
        body,
        mesh=split,
        in_specs=placed,
        out_specs=(P(SUB, None, "harm"), P(SUB, "harm", None), P(SUB, "harm", None)),
        check_vma=False,
    )
```

```python
import jax
import jax.numpy as jnp
from jax import lax
from jax.sharding import Mesh
from jax.sharding import PartitionSpec as P

SUB = ("sub_0", "sub_1", "sub_2")
PLANE = ("sub_0", "sub_1")
PAIR = ("sub_2", "harm")


def copy_for_each(x, axis):
    length = lax.axis_size(axis)
    return lax.all_to_all(jnp.broadcast_to(x[None], (length, *x.shape)), axis, 0, 0, tiled=True)


def joined_along(tiles, dim):
    tiles = jnp.moveaxis(tiles, 0, dim)
    shape = tiles.shape
    return tiles.reshape(*shape[:dim], shape[dim] * shape[dim + 1], *shape[dim + 2 :])


def whole_of(x, axes, dim):
    far, near = axes
    tiles = copy_for_each(copy_for_each(x, far), near)
    return joined_along(tiles.swapaxes(0, 1).reshape(-1, *x.shape), dim)


def collect(x, axis, dim):
    tiles = copy_for_each(x, axis)
    return joined_along(tiles, dim)


def in_blocks(x, dim, length):
    shape = x.shape
    tiles = x.reshape(*shape[:dim], length, shape[dim] // length, *shape[dim + 1 :])
    return jnp.moveaxis(tiles, dim, 0)


def sent_and_summed(x, axis, dim):
    tiles = in_blocks(x, dim, lax.axis_size(axis))
    arrived = lax.all_to_all(tiles, axis, split_axis=0, concat_axis=0, tiled=True)
    return arrived.astype(jnp.float32).sum(axis=0)


def body(
    lengths, owners, front_inverse, coupling, stiffness, displacement, forcing, lumped_mass, damping
):
    nharm = lax.axis_size("harm")
    harm_idx = lax.axis_index("harm")
    front_q = coupling.shape[1]
    width = coupling.shape[2]
    width_q = stiffness.shape[1]
    nown = lax.axis_size(SUB)
    own_rows = harm_idx * front_q + jnp.arange(front_q, dtype=jnp.int32)
    live_rows = own_rows[None, :] < lengths[:, None]
    masked = jnp.where(live_rows[:, :, None], coupling, jnp.zeros_like(coupling))
    longest = jnp.max(lengths)
    empty = jnp.zeros((masked.shape[0], front_q, width), jnp.float32)
    piece = lax.all_gather(masked, "harm", axis=1, tiled=True)
    modes = lax.cond(
        jnp.int32(0) < longest,
        lambda: jnp.einsum(
            "sfg,sgn->sfn", front_inverse, piece, preferred_element_type=jnp.float32
        ),
        lambda: empty,
    ).astype(jnp.bfloat16)
    nplane = lax.axis_size(PLANE)
    rows_q = displacement.shape[1]
    core = lax.axis_index("sub_2")
    near = (lax.axis_index(SUB) + nown // 2) % nown
    third = owners[2, 0]
    other = lax.ppermute(owners[2:3, 0], "sub_2", [(0, 1), (1, 0)])[0]
    plane = copy_for_each(displacement[0], PLANE)
    lent = lax.ppermute(
        lax.dynamic_index_in_dim(plane, other // 2, 0, keepdims=False), "sub_2", [(0, 1), (1, 0)]
    )
    here = lax.dynamic_index_in_dim(plane, third // 2, 0, keepdims=False)
    picked = jnp.stack(
        [
            lax.dynamic_index_in_dim(plane, near // 2, 0, keepdims=False),
            jnp.where(third % 2 == core, here, lent),
        ]
    )
    own_pair = collect(picked, "harm", 1)
    own_disp = jnp.stack([own_pair[0], own_pair[0], own_pair[1]])
    inner = -jnp.einsum("sfn,shn->shf", modes, own_disp, preferred_element_type=jnp.float32)
    interior = jnp.where(live_rows[:, None, :], inner, jnp.float32(0.0)).astype(jnp.bfloat16)
    disp_cols = lax.dynamic_slice_in_dim(own_disp, harm_idx * width_q, width_q, 2)
    contrib = jnp.einsum("shf,sfn->shn", interior, masked, preferred_element_type=jnp.float32)
    contrib = contrib + jnp.einsum(
        "shj,sjn->shn", disp_cols, stiffness, preferred_element_type=jnp.float32
    )
    near_c = (contrib[0] + contrib[1]).reshape(nharm, rows_q, width)
    third_c = contrib[2].reshape(nharm, rows_q, width)
    zero_rows = jnp.zeros_like(near_c)
    send = jnp.stack(
        [
            jnp.stack(
                [
                    jnp.where(peer_core == core, near_c, zero_rows),
                    jnp.where(third % 2 == peer_core, third_c, zero_rows),
                ],
                axis=1,
            )
            for peer_core in range(2)
        ]
    )
    came = lax.all_to_all(
        send.reshape(2 * nharm, 2, rows_q, width).astype(jnp.bfloat16), PAIR, 0, 0, tiled=True
    ).astype(jnp.float32)
    came = came.reshape(2, nharm, 2, rows_q, width).sum(axis=1)
    mine = jnp.where(core == 0, came[0], came[1])
    theirs = jnp.where(core == 0, came[1], came[0])
    near_part = mine[0]
    third_part = mine[1]
    other_part = theirs[1]
    slots = jnp.arange(nplane, dtype=jnp.int32)[:, None, None]
    dense = (
        jnp.where(slots == near // 2, near_part, jnp.float32(0.0))
        + jnp.where((slots == third // 2) & (third % 2 == core), third_part, jnp.float32(0.0))
        + jnp.where((slots == other // 2) & (other % 2 == core), other_part, jnp.float32(0.0))
    )
    arrived = lax.all_to_all(
        dense.astype(jnp.bfloat16), PLANE, split_axis=0, concat_axis=0, tiled=True
    ).astype(jnp.float32)
    gathered = jnp.sum(arrived, axis=0, keepdims=True)
    rows_q = displacement.shape[1]
    pairs_all = rows_q * nharm // 2
    rows = harm_idx * rows_q + jnp.arange(rows_q, dtype=jnp.int32)
    pair = (rows // 2).astype(jnp.float32)
    parity = (rows % 2).astype(jnp.float32)
    freq = 1.5 * (pair + 1.0) / pairs_all
    sign = 1.0 - 2.0 * parity
    disp = displacement.astype(jnp.float32)
    partner = disp.reshape(1, rows_q // 2, 2, width)[:, :, ::-1, :].reshape(1, rows_q, width)
    residual = (
        gathered
        - (freq * freq)[None, :, None] * lumped_mass[:, None, :] * disp
        + (sign * freq)[None, :, None] * damping[:, None, :] * partner
        - forcing
    )
    return (interior, residual, modes)


def solution(mesh):
    split = Mesh(
        mesh.devices.reshape(8, 8, 2, mesh.shape["harm"]), ("sub_0", "sub_1", "sub_2", "harm")
    )
    placed = (
        P(SUB),
        P(SUB, None),
        P(SUB, "harm", None),
        P(SUB, "harm", None),
        P(SUB, "harm", None),
        P(SUB, "harm", None),
        P(SUB, "harm", None),
        P(SUB, None),
        P(SUB, None),
    )
    return jax.shard_map(
        body,
        mesh=split,
        in_specs=placed,
        out_specs=(P(SUB, None, "harm"), P(SUB, "harm", None), P(SUB, "harm", None)),
        check_vma=False,
    )
```

```python
import jax
import jax.numpy as jnp
from jax import lax
from jax.sharding import Mesh
from jax.sharding import PartitionSpec as P

SUB = ("sub_0", "sub_1", "sub_2")
PLANE = ("sub_0", "sub_1")
PAIR = ("sub_2", "harm")


def copy_for_each(x, axis):
    length = lax.axis_size(axis)
    return lax.all_to_all(jnp.broadcast_to(x[None], (length, *x.shape)), axis, 0, 0, tiled=True)


def joined_along(tiles, dim):
    tiles = jnp.moveaxis(tiles, 0, dim)
    shape = tiles.shape
    return tiles.reshape(*shape[:dim], shape[dim] * shape[dim + 1], *shape[dim + 2 :])


def whole_of(x, axes, dim):
    far, near = axes
    tiles = copy_for_each(copy_for_each(x, far), near)
    return joined_along(tiles.swapaxes(0, 1).reshape(-1, *x.shape), dim)


def collect(x, axis, dim):
    tiles = copy_for_each(x, axis)
    return joined_along(tiles, dim)


def in_blocks(x, dim, length):
    shape = x.shape
    tiles = x.reshape(*shape[:dim], length, shape[dim] // length, *shape[dim + 1 :])
    return jnp.moveaxis(tiles, dim, 0)


def sent_and_summed(x, axis, dim):
    tiles = in_blocks(x, dim, lax.axis_size(axis))
    arrived = lax.all_to_all(tiles, axis, split_axis=0, concat_axis=0, tiled=True)
    return arrived.astype(jnp.float32).sum(axis=0)


def body(
    lengths, owners, front_inverse, coupling, stiffness, displacement, forcing, lumped_mass, damping
):
    nharm = lax.axis_size("harm")
    harm_idx = lax.axis_index("harm")
    front_q = coupling.shape[1]
    width = coupling.shape[2]
    width_q = stiffness.shape[1]
    nown = lax.axis_size(SUB)
    own_rows = harm_idx * front_q + jnp.arange(front_q, dtype=jnp.int32)
    live_rows = own_rows[None, :] < lengths[:, None]
    masked = jnp.where(live_rows[:, :, None], coupling, jnp.zeros_like(coupling))
    piece = lax.all_gather(coupling, "harm", axis=1, tiled=True)
    live_cols = jnp.arange(nharm * front_q, dtype=jnp.int32)[None, :] < lengths[:, None]
    front_live = jnp.where(live_cols[:, None, :], front_inverse, jnp.zeros_like(front_inverse))
    modes = jnp.einsum(
        "sfg,sgn->sfn", front_live, piece, preferred_element_type=jnp.float32
    ).astype(jnp.bfloat16)
    nplane = lax.axis_size(PLANE)
    rows_q = displacement.shape[1]
    core = lax.axis_index("sub_2")
    near = (lax.axis_index(SUB) + nown // 2) % nown
    third = owners[2, 0]
    other = lax.ppermute(owners[2:3, 0], "sub_2", [(0, 1), (1, 0)])[0]
    plane = copy_for_each(displacement[0], PLANE)
    lent = lax.ppermute(
        lax.dynamic_index_in_dim(plane, other // 2, 0, keepdims=False), "sub_2", [(0, 1), (1, 0)]
    )
    here = lax.dynamic_index_in_dim(plane, third // 2, 0, keepdims=False)
    picked = jnp.stack(
        [
            lax.dynamic_index_in_dim(plane, near // 2, 0, keepdims=False),
            jnp.where(third % 2 == core, here, lent),
        ]
    )
    own_pair = collect(picked, "harm", 1)
    own_disp = jnp.stack([own_pair[0], own_pair[0], own_pair[1]])
    inner = -jnp.einsum("sfn,shn->shf", modes, own_disp, preferred_element_type=jnp.float32)
    interior = jnp.where(live_rows[:, None, :], inner, jnp.float32(0.0)).astype(jnp.bfloat16)
    disp_cols = lax.dynamic_slice_in_dim(own_disp, harm_idx * width_q, width_q, 2)
    contrib = jnp.einsum("shf,sfn->shn", interior, masked, preferred_element_type=jnp.float32)
    contrib = contrib + jnp.einsum(
        "shj,sjn->shn", disp_cols, stiffness, preferred_element_type=jnp.float32
    )
    near_c = (contrib[0] + contrib[1]).reshape(nharm, rows_q, width)
    third_c = contrib[2].reshape(nharm, rows_q, width)
    zero_rows = jnp.zeros_like(near_c)
    send = jnp.stack(
        [
            jnp.stack(
                [
                    jnp.where(peer_core == core, near_c, zero_rows),
                    jnp.where(third % 2 == peer_core, third_c, zero_rows),
                ],
                axis=1,
            )
            for peer_core in range(2)
        ]
    )
    came = lax.all_to_all(
        send.reshape(2 * nharm, 2, rows_q, width).astype(jnp.bfloat16), PAIR, 0, 0, tiled=True
    ).astype(jnp.float32)
    came = came.reshape(2, nharm, 2, rows_q, width).sum(axis=1)
    mine = jnp.where(core == 0, came[0], came[1])
    theirs = jnp.where(core == 0, came[1], came[0])
    near_part = mine[0]
    third_part = mine[1]
    other_part = theirs[1]
    slots = jnp.arange(nplane, dtype=jnp.int32)[:, None, None]
    dense = (
        jnp.where(slots == near // 2, near_part, jnp.float32(0.0))
        + jnp.where((slots == third // 2) & (third % 2 == core), third_part, jnp.float32(0.0))
        + jnp.where((slots == other // 2) & (other % 2 == core), other_part, jnp.float32(0.0))
    )
    arrived = lax.all_to_all(
        dense.astype(jnp.bfloat16), PLANE, split_axis=0, concat_axis=0, tiled=True
    ).astype(jnp.float32)
    gathered = jnp.sum(arrived, axis=0, keepdims=True)
    rows_q = displacement.shape[1]
    pairs_all = rows_q * nharm // 2
    rows = harm_idx * rows_q + jnp.arange(rows_q, dtype=jnp.int32)
    pair = (rows // 2).astype(jnp.float32)
    parity = (rows % 2).astype(jnp.float32)
    freq = 1.5 * (pair + 1.0) / pairs_all
    sign = 1.0 - 2.0 * parity
    disp = displacement.astype(jnp.float32)
    partner = disp.reshape(1, rows_q // 2, 2, width)[:, :, ::-1, :].reshape(1, rows_q, width)
    residual = (
        gathered
        - (freq * freq)[None, :, None] * lumped_mass[:, None, :] * disp
        + (sign * freq)[None, :, None] * damping[:, None, :] * partner
        - forcing
    )
    return (interior, residual, modes)


def solution(mesh):
    split = Mesh(
        mesh.devices.reshape(8, 8, 2, mesh.shape["harm"]), ("sub_0", "sub_1", "sub_2", "harm")
    )
    placed = (
        P(SUB),
        P(SUB, None),
        P(SUB, "harm", None),
        P(SUB, "harm", None),
        P(SUB, "harm", None),
        P(SUB, "harm", None),
        P(SUB, "harm", None),
        P(SUB, None),
        P(SUB, None),
    )
    return jax.shard_map(
        body,
        mesh=split,
        in_specs=placed,
        out_specs=(P(SUB, None, "harm"), P(SUB, "harm", None), P(SUB, "harm", None)),
        check_vma=False,
    )
```

```python
import jax
import jax.numpy as jnp
from jax import lax
from jax.sharding import Mesh
from jax.sharding import PartitionSpec as P

SUB = ("sub_0", "sub_1", "sub_2")
PLANE = ("sub_0", "sub_1")
PAIR = ("sub_2", "harm")


def copy_for_each(x, axis):
    length = lax.axis_size(axis)
    return lax.all_to_all(jnp.broadcast_to(x[None], (length, *x.shape)), axis, 0, 0, tiled=True)


def joined_along(tiles, dim):
    tiles = jnp.moveaxis(tiles, 0, dim)
    shape = tiles.shape
    return tiles.reshape(*shape[:dim], shape[dim] * shape[dim + 1], *shape[dim + 2 :])


def whole_of(x, axes, dim):
    far, near = axes
    tiles = copy_for_each(copy_for_each(x, far), near)
    return joined_along(tiles.swapaxes(0, 1).reshape(-1, *x.shape), dim)


def collect(x, axis, dim):
    tiles = copy_for_each(x, axis)
    return joined_along(tiles, dim)


def in_blocks(x, dim, length):
    shape = x.shape
    tiles = x.reshape(*shape[:dim], length, shape[dim] // length, *shape[dim + 1 :])
    return jnp.moveaxis(tiles, dim, 0)


def sent_and_summed(x, axis, dim):
    tiles = in_blocks(x, dim, lax.axis_size(axis))
    arrived = lax.all_to_all(tiles, axis, split_axis=0, concat_axis=0, tiled=True)
    return arrived.astype(jnp.float32).sum(axis=0)


def body(
    lengths, owners, front_inverse, coupling, stiffness, displacement, forcing, lumped_mass, damping
):
    nharm = lax.axis_size("harm")
    harm_idx = lax.axis_index("harm")
    front_q = coupling.shape[1]
    width = coupling.shape[2]
    width_q = stiffness.shape[1]
    nown = lax.axis_size(SUB)
    own_rows = harm_idx * front_q + jnp.arange(front_q, dtype=jnp.int32)
    live_rows = own_rows[None, :] < lengths[:, None]
    masked = jnp.where(live_rows[:, :, None], coupling, jnp.zeros_like(coupling))
    piece = lax.all_gather(coupling, "harm", axis=1, tiled=True)
    live_cols = jnp.arange(nharm * front_q, dtype=jnp.int32)[None, :] < lengths[:, None]
    front_live = jnp.where(live_cols[:, None, :], front_inverse, jnp.zeros_like(front_inverse))
    modes = jnp.einsum(
        "sfg,sgn->sfn", front_live, piece, preferred_element_type=jnp.float32
    ).astype(jnp.bfloat16)
    nplane = lax.axis_size(PLANE)
    rows_q = displacement.shape[1]
    core = lax.axis_index("sub_2")
    near = (lax.axis_index(SUB) + nown // 2) % nown
    third = owners[2, 0]
    other = lax.ppermute(owners[2:3, 0], "sub_2", [(0, 1), (1, 0)])[0]
    plane = copy_for_each(displacement[0], PLANE)
    lent = lax.ppermute(
        lax.dynamic_index_in_dim(plane, other // 2, 0, keepdims=False), "sub_2", [(0, 1), (1, 0)]
    )
    here = lax.dynamic_index_in_dim(plane, third // 2, 0, keepdims=False)
    picked = jnp.stack(
        [
            lax.dynamic_index_in_dim(plane, near // 2, 0, keepdims=False),
            jnp.where(third % 2 == core, here, lent),
        ]
    )
    own_pair = collect(picked, "harm", 1)
    own_disp = jnp.stack([own_pair[0], own_pair[0], own_pair[1]])
    whole_y = jnp.einsum("shn,sgn->shg", own_disp, piece, preferred_element_type=jnp.float32)
    whole_y = jnp.where(live_cols[:, None, :], whole_y, jnp.float32(0.0))
    inner = -jnp.einsum(
        "shg,sfg->shf",
        whole_y,
        front_inverse.astype(jnp.float32),
        precision=lax.Precision.HIGHEST,
        preferred_element_type=jnp.float32,
    )
    interior = jnp.where(live_rows[:, None, :], inner, jnp.float32(0.0)).astype(jnp.bfloat16)
    disp_cols = lax.dynamic_slice_in_dim(own_disp, harm_idx * width_q, width_q, 2)
    contrib = jnp.einsum("shf,sfn->shn", interior, masked, preferred_element_type=jnp.float32)
    contrib = contrib + jnp.einsum(
        "shj,sjn->shn", disp_cols, stiffness, preferred_element_type=jnp.float32
    )
    near_c = (contrib[0] + contrib[1]).reshape(nharm, rows_q, width)
    third_c = contrib[2].reshape(nharm, rows_q, width)
    zero_rows = jnp.zeros_like(near_c)
    send = jnp.stack(
        [
            jnp.stack(
                [
                    jnp.where(peer_core == core, near_c, zero_rows),
                    jnp.where(third % 2 == peer_core, third_c, zero_rows),
                ],
                axis=1,
            )
            for peer_core in range(2)
        ]
    )
    came = lax.all_to_all(
        send.reshape(2 * nharm, 2, rows_q, width).astype(jnp.bfloat16), PAIR, 0, 0, tiled=True
    ).astype(jnp.float32)
    came = came.reshape(2, nharm, 2, rows_q, width).sum(axis=1)
    mine = jnp.where(core == 0, came[0], came[1])
    theirs = jnp.where(core == 0, came[1], came[0])
    near_part = mine[0]
    third_part = mine[1]
    other_part = theirs[1]
    slots = jnp.arange(nplane, dtype=jnp.int32)[:, None, None]
    dense = (
        jnp.where(slots == near // 2, near_part, jnp.float32(0.0))
        + jnp.where((slots == third // 2) & (third % 2 == core), third_part, jnp.float32(0.0))
        + jnp.where((slots == other // 2) & (other % 2 == core), other_part, jnp.float32(0.0))
    )
    arrived = lax.all_to_all(
        dense.astype(jnp.bfloat16), PLANE, split_axis=0, concat_axis=0, tiled=True
    ).astype(jnp.float32)
    gathered = jnp.sum(arrived, axis=0, keepdims=True)
    rows_q = displacement.shape[1]
    pairs_all = rows_q * nharm // 2
    rows = harm_idx * rows_q + jnp.arange(rows_q, dtype=jnp.int32)
    pair = (rows // 2).astype(jnp.float32)
    parity = (rows % 2).astype(jnp.float32)
    freq = 1.5 * (pair + 1.0) / pairs_all
    sign = 1.0 - 2.0 * parity
    disp = displacement.astype(jnp.float32)
    partner = disp.reshape(1, rows_q // 2, 2, width)[:, :, ::-1, :].reshape(1, rows_q, width)
    residual = (
        gathered
        - (freq * freq)[None, :, None] * lumped_mass[:, None, :] * disp
        + (sign * freq)[None, :, None] * damping[:, None, :] * partner
        - forcing
    )
    return (interior, residual, modes)


def solution(mesh):
    split = Mesh(
        mesh.devices.reshape(8, 8, 2, mesh.shape["harm"]), ("sub_0", "sub_1", "sub_2", "harm")
    )
    placed = (
        P(SUB),
        P(SUB, None),
        P(SUB, "harm", None),
        P(SUB, "harm", None),
        P(SUB, "harm", None),
        P(SUB, "harm", None),
        P(SUB, "harm", None),
        P(SUB, None),
        P(SUB, None),
    )
    return jax.shard_map(
        body,
        mesh=split,
        in_specs=placed,
        out_specs=(P(SUB, None, "harm"), P(SUB, "harm", None), P(SUB, "harm", None)),
        check_vma=False,
    )
```

```python
import jax
import jax.numpy as jnp
from jax import lax
from jax.sharding import Mesh
from jax.sharding import PartitionSpec as P

SUB = ("sub_0", "sub_1", "sub_2")
PLANE = ("sub_0", "sub_1")
PAIR = ("sub_2", "harm")


def copy_for_each(x, axis):
    length = lax.axis_size(axis)
    return lax.all_to_all(jnp.broadcast_to(x[None], (length, *x.shape)), axis, 0, 0, tiled=True)


def joined_along(tiles, dim):
    tiles = jnp.moveaxis(tiles, 0, dim)
    shape = tiles.shape
    return tiles.reshape(*shape[:dim], shape[dim] * shape[dim + 1], *shape[dim + 2 :])


def whole_of(x, axes, dim):
    far, near = axes
    tiles = copy_for_each(copy_for_each(x, far), near)
    return joined_along(tiles.swapaxes(0, 1).reshape(-1, *x.shape), dim)


def collect(x, axis, dim):
    tiles = copy_for_each(x, axis)
    return joined_along(tiles, dim)


def in_blocks(x, dim, length):
    shape = x.shape
    tiles = x.reshape(*shape[:dim], length, shape[dim] // length, *shape[dim + 1 :])
    return jnp.moveaxis(tiles, dim, 0)


def sent_and_summed(x, axis, dim):
    tiles = in_blocks(x, dim, lax.axis_size(axis))
    arrived = lax.all_to_all(tiles, axis, split_axis=0, concat_axis=0, tiled=True)
    return arrived.astype(jnp.float32).sum(axis=0)


def body(
    lengths, owners, front_inverse, coupling, stiffness, displacement, forcing, lumped_mass, damping
):
    nharm = lax.axis_size("harm")
    harm_idx = lax.axis_index("harm")
    front_q = coupling.shape[1]
    width = coupling.shape[2]
    width_q = stiffness.shape[1]
    nown = lax.axis_size(SUB)
    own_rows = harm_idx * front_q + jnp.arange(front_q, dtype=jnp.int32)
    live_rows = own_rows[None, :] < lengths[:, None]
    masked = jnp.where(live_rows[:, :, None], coupling, jnp.zeros_like(coupling))
    piece = lax.all_gather(coupling, "harm", axis=1, tiled=True)
    live_cols = jnp.arange(nharm * front_q, dtype=jnp.int32)[None, :] < lengths[:, None]
    front_live = jnp.where(live_cols[:, None, :], front_inverse, jnp.zeros_like(front_inverse))
    modes = jnp.einsum(
        "sfg,sgn->sfn", front_live, piece, preferred_element_type=jnp.float32
    ).astype(jnp.bfloat16)
    nplane = lax.axis_size(PLANE)
    rows_q = displacement.shape[1]
    core = lax.axis_index("sub_2")
    near = (lax.axis_index(SUB) + nown // 2) % nown
    third = owners[2, 0]
    other = lax.ppermute(owners[2:3, 0], "sub_2", [(0, 1), (1, 0)])[0]
    plane = copy_for_each(displacement[0], PLANE)
    lent = lax.ppermute(
        lax.dynamic_index_in_dim(plane, other // 2, 0, keepdims=False), "sub_2", [(0, 1), (1, 0)]
    )
    here = lax.dynamic_index_in_dim(plane, third // 2, 0, keepdims=False)
    picked = jnp.stack(
        [
            lax.dynamic_index_in_dim(plane, near // 2, 0, keepdims=False),
            jnp.where(third % 2 == core, here, lent),
        ]
    )
    own_pair = collect(picked, "harm", 1)
    own_disp = jnp.stack([own_pair[0], own_pair[0], own_pair[1]])
    whole_y = jnp.einsum("shn,sgn->shg", own_disp, piece, preferred_element_type=jnp.float32)
    whole_y = jnp.where(live_cols[:, None, :], whole_y, jnp.float32(0.0))
    inner = -jnp.einsum(
        "shg,sfg->shf",
        whole_y,
        front_inverse.astype(jnp.float32),
        precision=lax.Precision.HIGH,
        preferred_element_type=jnp.float32,
    )
    interior = jnp.where(live_rows[:, None, :], inner, jnp.float32(0.0)).astype(jnp.bfloat16)
    disp_cols = lax.dynamic_slice_in_dim(own_disp, harm_idx * width_q, width_q, 2)
    contrib = jnp.einsum("shf,sfn->shn", interior, masked, preferred_element_type=jnp.float32)
    contrib = contrib + jnp.einsum(
        "shj,sjn->shn", disp_cols, stiffness, preferred_element_type=jnp.float32
    )
    near_c = (contrib[0] + contrib[1]).reshape(nharm, rows_q, width)
    third_c = contrib[2].reshape(nharm, rows_q, width)
    zero_rows = jnp.zeros_like(near_c)
    send = jnp.stack(
        [
            jnp.stack(
                [
                    jnp.where(peer_core == core, near_c, zero_rows),
                    jnp.where(third % 2 == peer_core, third_c, zero_rows),
                ],
                axis=1,
            )
            for peer_core in range(2)
        ]
    )
    came = lax.all_to_all(
        send.reshape(2 * nharm, 2, rows_q, width).astype(jnp.bfloat16), PAIR, 0, 0, tiled=True
    ).astype(jnp.float32)
    came = came.reshape(2, nharm, 2, rows_q, width).sum(axis=1)
    mine = jnp.where(core == 0, came[0], came[1])
    theirs = jnp.where(core == 0, came[1], came[0])
    near_part = mine[0]
    third_part = mine[1]
    other_part = theirs[1]
    slots = jnp.arange(nplane, dtype=jnp.int32)[:, None, None]
    dense = (
        jnp.where(slots == near // 2, near_part, jnp.float32(0.0))
        + jnp.where((slots == third // 2) & (third % 2 == core), third_part, jnp.float32(0.0))
        + jnp.where((slots == other // 2) & (other % 2 == core), other_part, jnp.float32(0.0))
    )
    arrived = lax.all_to_all(
        dense.astype(jnp.bfloat16), PLANE, split_axis=0, concat_axis=0, tiled=True
    ).astype(jnp.float32)
    gathered = jnp.sum(arrived, axis=0, keepdims=True)
    rows_q = displacement.shape[1]
    pairs_all = rows_q * nharm // 2
    rows = harm_idx * rows_q + jnp.arange(rows_q, dtype=jnp.int32)
    pair = (rows // 2).astype(jnp.float32)
    parity = (rows % 2).astype(jnp.float32)
    freq = 1.5 * (pair + 1.0) / pairs_all
    sign = 1.0 - 2.0 * parity
    disp = displacement.astype(jnp.float32)
    partner = disp.reshape(1, rows_q // 2, 2, width)[:, :, ::-1, :].reshape(1, rows_q, width)
    residual = (
        gathered
        - (freq * freq)[None, :, None] * lumped_mass[:, None, :] * disp
        + (sign * freq)[None, :, None] * damping[:, None, :] * partner
        - forcing
    )
    return (interior, residual, modes)


def solution(mesh):
    split = Mesh(
        mesh.devices.reshape(8, 8, 2, mesh.shape["harm"]), ("sub_0", "sub_1", "sub_2", "harm")
    )
    placed = (
        P(SUB),
        P(SUB, None),
        P(SUB, "harm", None),
        P(SUB, "harm", None),
        P(SUB, "harm", None),
        P(SUB, "harm", None),
        P(SUB, "harm", None),
        P(SUB, None),
        P(SUB, None),
    )
    return jax.shard_map(
        body,
        mesh=split,
        in_specs=placed,
        out_specs=(P(SUB, None, "harm"), P(SUB, "harm", None), P(SUB, "harm", None)),
        check_vma=False,
    )
```

```python
import jax
import jax.numpy as jnp
from jax import lax
from jax.sharding import Mesh
from jax.sharding import PartitionSpec as P

SUB = ("sub_0", "sub_1", "sub_2")
PLANE = ("sub_0", "sub_1")
PAIR = ("sub_2", "harm")


def copy_for_each(x, axis):
    length = lax.axis_size(axis)
    return lax.all_to_all(jnp.broadcast_to(x[None], (length, *x.shape)), axis, 0, 0, tiled=True)


def joined_along(tiles, dim):
    tiles = jnp.moveaxis(tiles, 0, dim)
    shape = tiles.shape
    return tiles.reshape(*shape[:dim], shape[dim] * shape[dim + 1], *shape[dim + 2 :])


def whole_of(x, axes, dim):
    far, near = axes
    tiles = copy_for_each(copy_for_each(x, far), near)
    return joined_along(tiles.swapaxes(0, 1).reshape(-1, *x.shape), dim)


def collect(x, axis, dim):
    tiles = copy_for_each(x, axis)
    return joined_along(tiles, dim)


def in_blocks(x, dim, length):
    shape = x.shape
    tiles = x.reshape(*shape[:dim], length, shape[dim] // length, *shape[dim + 1 :])
    return jnp.moveaxis(tiles, dim, 0)


def sent_and_summed(x, axis, dim):
    tiles = in_blocks(x, dim, lax.axis_size(axis))
    arrived = lax.all_to_all(tiles, axis, split_axis=0, concat_axis=0, tiled=True)
    return arrived.astype(jnp.float32).sum(axis=0)


def body(
    lengths, owners, front_inverse, coupling, stiffness, displacement, forcing, lumped_mass, damping
):
    nharm = lax.axis_size("harm")
    harm_idx = lax.axis_index("harm")
    front_q = coupling.shape[1]
    width = coupling.shape[2]
    width_q = stiffness.shape[1]
    nown = lax.axis_size(SUB)
    own_rows = harm_idx * front_q + jnp.arange(front_q, dtype=jnp.int32)
    live_rows = own_rows[None, :] < lengths[:, None]
    masked = jnp.where(live_rows[:, :, None], coupling, jnp.zeros_like(coupling))
    piece = lax.all_gather(coupling, "harm", axis=1, tiled=True)
    live_cols = jnp.arange(nharm * front_q, dtype=jnp.int32)[None, :] < lengths[:, None]
    front_live = jnp.where(live_cols[:, None, :], front_inverse, jnp.zeros_like(front_inverse))
    modes = jnp.einsum(
        "sfg,sgn->sfn", front_live, piece, preferred_element_type=jnp.float32
    ).astype(jnp.bfloat16)
    nplane = lax.axis_size(PLANE)
    rows_q = displacement.shape[1]
    core = lax.axis_index("sub_2")
    near = (lax.axis_index(SUB) + nown // 2) % nown
    third = owners[2, 0]
    other = lax.ppermute(owners[2:3, 0], "sub_2", [(0, 1), (1, 0)])[0]
    plane = copy_for_each(displacement[0], PLANE)
    lent = lax.ppermute(
        lax.dynamic_index_in_dim(plane, other // 2, 0, keepdims=False), "sub_2", [(0, 1), (1, 0)]
    )
    here = lax.dynamic_index_in_dim(plane, third // 2, 0, keepdims=False)
    picked = jnp.stack(
        [
            lax.dynamic_index_in_dim(plane, near // 2, 0, keepdims=False),
            jnp.where(third % 2 == core, here, lent),
        ]
    )
    own_pair = collect(picked, "harm", 1)
    own_disp = jnp.stack([own_pair[0], own_pair[0], own_pair[1]])
    whole_y = jnp.einsum("shn,sgn->shg", own_disp, piece, preferred_element_type=jnp.float32)
    whole_y = jnp.where(live_cols[:, None, :], whole_y, jnp.float32(0.0))
    inner = -jnp.einsum(
        "shg,sfg->shf", whole_y.astype(jnp.bfloat16), front_inverse, preferred_element_type=jnp.float32
    )
    interior = jnp.where(live_rows[:, None, :], inner, jnp.float32(0.0)).astype(jnp.bfloat16)
    disp_cols = lax.dynamic_slice_in_dim(own_disp, harm_idx * width_q, width_q, 2)
    contrib = jnp.einsum("shf,sfn->shn", interior, masked, preferred_element_type=jnp.float32)
    contrib = contrib + jnp.einsum(
        "shj,sjn->shn", disp_cols, stiffness, preferred_element_type=jnp.float32
    )
    near_c = (contrib[0] + contrib[1]).reshape(nharm, rows_q, width)
    third_c = contrib[2].reshape(nharm, rows_q, width)
    zero_rows = jnp.zeros_like(near_c)
    send = jnp.stack(
        [
            jnp.stack(
                [
                    jnp.where(peer_core == core, near_c, zero_rows),
                    jnp.where(third % 2 == peer_core, third_c, zero_rows),
                ],
                axis=1,
            )
            for peer_core in range(2)
        ]
    )
    came = lax.all_to_all(
        send.reshape(2 * nharm, 2, rows_q, width).astype(jnp.bfloat16), PAIR, 0, 0, tiled=True
    ).astype(jnp.float32)
    came = came.reshape(2, nharm, 2, rows_q, width).sum(axis=1)
    mine = jnp.where(core == 0, came[0], came[1])
    theirs = jnp.where(core == 0, came[1], came[0])
    near_part = mine[0]
    third_part = mine[1]
    other_part = theirs[1]
    slots = jnp.arange(nplane, dtype=jnp.int32)[:, None, None]
    dense = (
        jnp.where(slots == near // 2, near_part, jnp.float32(0.0))
        + jnp.where((slots == third // 2) & (third % 2 == core), third_part, jnp.float32(0.0))
        + jnp.where((slots == other // 2) & (other % 2 == core), other_part, jnp.float32(0.0))
    )
    arrived = lax.all_to_all(
        dense.astype(jnp.bfloat16), PLANE, split_axis=0, concat_axis=0, tiled=True
    ).astype(jnp.float32)
    gathered = jnp.sum(arrived, axis=0, keepdims=True)
    rows_q = displacement.shape[1]
    pairs_all = rows_q * nharm // 2
    rows = harm_idx * rows_q + jnp.arange(rows_q, dtype=jnp.int32)
    pair = (rows // 2).astype(jnp.float32)
    parity = (rows % 2).astype(jnp.float32)
    freq = 1.5 * (pair + 1.0) / pairs_all
    sign = 1.0 - 2.0 * parity
    disp = displacement.astype(jnp.float32)
    partner = disp.reshape(1, rows_q // 2, 2, width)[:, :, ::-1, :].reshape(1, rows_q, width)
    residual = (
        gathered
        - (freq * freq)[None, :, None] * lumped_mass[:, None, :] * disp
        + (sign * freq)[None, :, None] * damping[:, None, :] * partner
        - forcing
    )
    return (interior, residual, modes)


def solution(mesh):
    split = Mesh(
        mesh.devices.reshape(8, 8, 2, mesh.shape["harm"]), ("sub_0", "sub_1", "sub_2", "harm")
    )
    placed = (
        P(SUB),
        P(SUB, None),
        P(SUB, "harm", None),
        P(SUB, "harm", None),
        P(SUB, "harm", None),
        P(SUB, "harm", None),
        P(SUB, "harm", None),
        P(SUB, None),
        P(SUB, None),
    )
    return jax.shard_map(
        body,
        mesh=split,
        in_specs=placed,
        out_specs=(P(SUB, None, "harm"), P(SUB, "harm", None), P(SUB, "harm", None)),
        check_vma=False,
    )
```

```python
import jax
import jax.numpy as jnp
from jax import lax
from jax.sharding import Mesh
from jax.sharding import PartitionSpec as P

SUB = ("sub_0", "sub_1", "sub_2")
PLANE = ("sub_0", "sub_1")
PAIR = ("sub_2", "harm")


def copy_for_each(x, axis):
    length = lax.axis_size(axis)
    return lax.all_to_all(jnp.broadcast_to(x[None], (length, *x.shape)), axis, 0, 0, tiled=True)


def joined_along(tiles, dim):
    tiles = jnp.moveaxis(tiles, 0, dim)
    shape = tiles.shape
    return tiles.reshape(*shape[:dim], shape[dim] * shape[dim + 1], *shape[dim + 2 :])


def whole_of(x, axes, dim):
    far, near = axes
    tiles = copy_for_each(copy_for_each(x, far), near)
    return joined_along(tiles.swapaxes(0, 1).reshape(-1, *x.shape), dim)


def collect(x, axis, dim):
    tiles = copy_for_each(x, axis)
    return joined_along(tiles, dim)


def in_blocks(x, dim, length):
    shape = x.shape
    tiles = x.reshape(*shape[:dim], length, shape[dim] // length, *shape[dim + 1 :])
    return jnp.moveaxis(tiles, dim, 0)


def sent_and_summed(x, axis, dim):
    tiles = in_blocks(x, dim, lax.axis_size(axis))
    arrived = lax.all_to_all(tiles, axis, split_axis=0, concat_axis=0, tiled=True)
    return arrived.astype(jnp.float32).sum(axis=0)


def body(
    lengths, owners, front_inverse, coupling, stiffness, displacement, forcing, lumped_mass, damping
):
    nharm = lax.axis_size("harm")
    harm_idx = lax.axis_index("harm")
    front_q = coupling.shape[1]
    width = coupling.shape[2]
    width_q = stiffness.shape[1]
    nown = lax.axis_size(SUB)
    own_rows = harm_idx * front_q + jnp.arange(front_q, dtype=jnp.int32)
    live_rows = own_rows[None, :] < lengths[:, None]
    masked = jnp.where(live_rows[:, :, None], coupling, jnp.zeros_like(coupling))
    piece = lax.all_gather(coupling, "harm", axis=1, tiled=True)
    live_cols = jnp.arange(nharm * front_q, dtype=jnp.int32)[None, :] < lengths[:, None]
    front_live = jnp.where(live_cols[:, None, :], front_inverse, jnp.zeros_like(front_inverse))
    modes = jnp.einsum(
        "sfg,sgn->sfn", front_live, piece, preferred_element_type=jnp.float32
    ).astype(jnp.bfloat16)
    nplane = lax.axis_size(PLANE)
    rows_q = displacement.shape[1]
    core = lax.axis_index("sub_2")
    near = (lax.axis_index(SUB) + nown // 2) % nown
    third = owners[2, 0]
    other = lax.ppermute(owners[2:3, 0], "sub_2", [(0, 1), (1, 0)])[0]
    plane = copy_for_each(displacement[0], PLANE)
    lent = lax.ppermute(
        lax.dynamic_index_in_dim(plane, other // 2, 0, keepdims=False), "sub_2", [(0, 1), (1, 0)]
    )
    here = lax.dynamic_index_in_dim(plane, third // 2, 0, keepdims=False)
    picked = jnp.stack(
        [
            lax.dynamic_index_in_dim(plane, near // 2, 0, keepdims=False),
            jnp.where(third % 2 == core, here, lent),
        ]
    )
    own_pair = collect(picked, "harm", 1)
    own_disp = jnp.stack([own_pair[0], own_pair[0], own_pair[1]])
    whole_y = jnp.einsum("shn,sgn->shg", own_disp, piece, preferred_element_type=jnp.float32)
    whole_y = jnp.where(live_cols[:, None, :], whole_y, jnp.float32(0.0))
    inner = -jnp.einsum(
        "shg,sfg->shf",
        whole_y,
        front_inverse.astype(jnp.float32),
        precision=lax.Precision.HIGH,
        preferred_element_type=jnp.float32,
    )
    interior = jnp.where(live_rows[:, None, :], inner, jnp.float32(0.0)).astype(jnp.bfloat16)
    disp_cols = lax.dynamic_slice_in_dim(own_disp, harm_idx * width_q, width_q, 2)
    contrib = jnp.einsum("shf,sfn->shn", interior, masked, preferred_element_type=jnp.float32)
    contrib = contrib + jnp.einsum(
        "shj,sjn->shn", disp_cols, stiffness, preferred_element_type=jnp.float32
    )
    near_c = (contrib[0] + contrib[1]).reshape(nharm, rows_q, width)
    third_c = contrib[2].reshape(nharm, rows_q, width)
    zero_rows = jnp.zeros_like(near_c)
    send = jnp.stack(
        [
            jnp.stack(
                [
                    jnp.where(peer_core == core, near_c, zero_rows),
                    jnp.where(third % 2 == peer_core, third_c, zero_rows),
                ],
                axis=1,
            )
            for peer_core in range(2)
        ]
    )
    came = lax.all_to_all(
        send.reshape(2 * nharm, 2, rows_q, width).astype(jnp.bfloat16), PAIR, 0, 0, tiled=True
    ).astype(jnp.float32)
    came = came.reshape(2, nharm, 2, rows_q, width).sum(axis=1)
    mine = jnp.where(core == 0, came[0], came[1])
    theirs = jnp.where(core == 0, came[1], came[0])
    near_part = mine[0]
    third_part = mine[1]
    other_part = theirs[1]
    dense = jnp.zeros((nplane, rows_q, width), jnp.bfloat16)
    for slot, part, valid in (
        (near // 2, near_part, True),
        (third // 2, third_part, third % 2 == core),
        (other // 2, other_part, other % 2 == core),
    ):
        held = lax.dynamic_index_in_dim(dense, slot, 0, keepdims=False).astype(jnp.float32)
        summed = jnp.where(valid, held + part, held).astype(jnp.bfloat16)
        dense = lax.dynamic_update_index_in_dim(dense, summed, slot, 0)
    arrived = lax.all_to_all(
        dense, PLANE, split_axis=0, concat_axis=0, tiled=True
    ).astype(jnp.float32)
    gathered = jnp.sum(arrived, axis=0, keepdims=True)
    rows_q = displacement.shape[1]
    pairs_all = rows_q * nharm // 2
    rows = harm_idx * rows_q + jnp.arange(rows_q, dtype=jnp.int32)
    pair = (rows // 2).astype(jnp.float32)
    parity = (rows % 2).astype(jnp.float32)
    freq = 1.5 * (pair + 1.0) / pairs_all
    sign = 1.0 - 2.0 * parity
    disp = displacement.astype(jnp.float32)
    partner = disp.reshape(1, rows_q // 2, 2, width)[:, :, ::-1, :].reshape(1, rows_q, width)
    residual = (
        gathered
        - (freq * freq)[None, :, None] * lumped_mass[:, None, :] * disp
        + (sign * freq)[None, :, None] * damping[:, None, :] * partner
        - forcing
    )
    return (interior, residual, modes)


def solution(mesh):
    split = Mesh(
        mesh.devices.reshape(8, 8, 2, mesh.shape["harm"]), ("sub_0", "sub_1", "sub_2", "harm")
    )
    placed = (
        P(SUB),
        P(SUB, None),
        P(SUB, "harm", None),
        P(SUB, "harm", None),
        P(SUB, "harm", None),
        P(SUB, "harm", None),
        P(SUB, "harm", None),
        P(SUB, None),
        P(SUB, None),
    )
    return jax.shard_map(
        body,
        mesh=split,
        in_specs=placed,
        out_specs=(P(SUB, None, "harm"), P(SUB, "harm", None), P(SUB, "harm", None)),
        check_vma=False,
    )
```

```python
import jax
import jax.numpy as jnp
from jax import lax
from jax.sharding import Mesh
from jax.sharding import PartitionSpec as P

SUB = ("sub_0", "sub_1", "sub_2")
PLANE = ("sub_0", "sub_1")
PAIR = ("sub_2", "harm")


def copy_for_each(x, axis):
    length = lax.axis_size(axis)
    return lax.all_to_all(jnp.broadcast_to(x[None], (length, *x.shape)), axis, 0, 0, tiled=True)


def joined_along(tiles, dim):
    tiles = jnp.moveaxis(tiles, 0, dim)
    shape = tiles.shape
    return tiles.reshape(*shape[:dim], shape[dim] * shape[dim + 1], *shape[dim + 2 :])


def whole_of(x, axes, dim):
    far, near = axes
    tiles = copy_for_each(copy_for_each(x, far), near)
    return joined_along(tiles.swapaxes(0, 1).reshape(-1, *x.shape), dim)


def collect(x, axis, dim):
    tiles = copy_for_each(x, axis)
    return joined_along(tiles, dim)


def in_blocks(x, dim, length):
    shape = x.shape
    tiles = x.reshape(*shape[:dim], length, shape[dim] // length, *shape[dim + 1 :])
    return jnp.moveaxis(tiles, dim, 0)


def sent_and_summed(x, axis, dim):
    tiles = in_blocks(x, dim, lax.axis_size(axis))
    arrived = lax.all_to_all(tiles, axis, split_axis=0, concat_axis=0, tiled=True)
    return arrived.astype(jnp.float32).sum(axis=0)


def body(
    lengths, owners, front_inverse, coupling, stiffness, displacement, forcing, lumped_mass, damping
):
    nharm = lax.axis_size("harm")
    harm_idx = lax.axis_index("harm")
    front_q = coupling.shape[1]
    width = coupling.shape[2]
    width_q = stiffness.shape[1]
    nown = lax.axis_size(SUB)
    own_rows = harm_idx * front_q + jnp.arange(front_q, dtype=jnp.int32)
    live_rows = own_rows[None, :] < lengths[:, None]
    masked = jnp.where(live_rows[:, :, None], coupling, jnp.zeros_like(coupling))
    piece = lax.all_gather(coupling, "harm", axis=1, tiled=True)
    live_cols = jnp.arange(nharm * front_q, dtype=jnp.int32)[None, :] < lengths[:, None]
    front_live = jnp.where(live_cols[:, None, :], front_inverse, jnp.zeros_like(front_inverse))
    modes = jnp.einsum(
        "sfg,sgn->sfn", front_live, piece, preferred_element_type=jnp.float32
    ).astype(jnp.bfloat16)
    nplane = lax.axis_size(PLANE)
    rows_q = displacement.shape[1]
    core = lax.axis_index("sub_2")
    near = (lax.axis_index(SUB) + nown // 2) % nown
    third = owners[2, 0]
    other = lax.ppermute(owners[2:3, 0], "sub_2", [(0, 1), (1, 0)])[0]
    plane = copy_for_each(displacement[0], PLANE)
    zero_block = jnp.zeros_like(plane[0])
    lend = []
    for peer_core in range(2):
        wanted = jnp.where(peer_core == core, third, other)
        lend.append(
            jnp.stack(
                [
                    jnp.where(
                        peer_core == core,
                        lax.dynamic_index_in_dim(plane, near // 2, 0, keepdims=False),
                        zero_block,
                    ),
                    jnp.where(
                        wanted % 2 == core,
                        lax.dynamic_index_in_dim(plane, wanted // 2, 0, keepdims=False),
                        zero_block,
                    ),
                ]
            )
        )
    lend = jnp.broadcast_to(jnp.stack(lend)[:, None], (2, nharm, 2, *zero_block.shape))
    lent = lax.all_to_all(
        lend.reshape(2 * nharm, 2, *zero_block.shape), PAIR, 0, 0, tiled=True
    ).reshape(2, nharm, 2, *zero_block.shape)
    lent = (lent[0] + lent[1]).transpose(1, 0, 2, 3)
    own_pair = lent.reshape(2, nharm * zero_block.shape[0], width)
    own_disp = jnp.stack([own_pair[0], own_pair[0], own_pair[1]])
    whole_y = jnp.einsum("shn,sgn->shg", own_disp, piece, preferred_element_type=jnp.float32)
    whole_y = jnp.where(live_cols[:, None, :], whole_y, jnp.float32(0.0))
    inner = -jnp.einsum(
        "shg,sfg->shf",
        whole_y,
        front_inverse.astype(jnp.float32),
        precision=lax.Precision.HIGH,
        preferred_element_type=jnp.float32,
    )
    interior = jnp.where(live_rows[:, None, :], inner, jnp.float32(0.0)).astype(jnp.bfloat16)
    disp_cols = lax.dynamic_slice_in_dim(own_disp, harm_idx * width_q, width_q, 2)
    contrib = jnp.einsum("shf,sfn->shn", interior, masked, preferred_element_type=jnp.float32)
    contrib = contrib + jnp.einsum(
        "shj,sjn->shn", disp_cols, stiffness, preferred_element_type=jnp.float32
    )
    near_c = (contrib[0] + contrib[1]).reshape(nharm, rows_q, width)
    third_c = contrib[2].reshape(nharm, rows_q, width)
    zero_rows = jnp.zeros_like(near_c)
    send = jnp.stack(
        [
            jnp.stack(
                [
                    jnp.where(peer_core == core, near_c, zero_rows),
                    jnp.where(third % 2 == peer_core, third_c, zero_rows),
                ],
                axis=1,
            )
            for peer_core in range(2)
        ]
    )
    came = lax.all_to_all(
        send.reshape(2 * nharm, 2, rows_q, width).astype(jnp.bfloat16), PAIR, 0, 0, tiled=True
    ).astype(jnp.float32)
    came = came.reshape(2, nharm, 2, rows_q, width).sum(axis=1)
    mine = jnp.where(core == 0, came[0], came[1])
    theirs = jnp.where(core == 0, came[1], came[0])
    near_part = mine[0]
    third_part = mine[1]
    other_part = theirs[1]
    slots = jnp.arange(nplane, dtype=jnp.int32)[:, None, None]
    dense = (
        jnp.where(slots == near // 2, near_part, jnp.float32(0.0))
        + jnp.where((slots == third // 2) & (third % 2 == core), third_part, jnp.float32(0.0))
        + jnp.where((slots == other // 2) & (other % 2 == core), other_part, jnp.float32(0.0))
    )
    arrived = lax.all_to_all(
        dense.astype(jnp.bfloat16), PLANE, split_axis=0, concat_axis=0, tiled=True
    ).astype(jnp.float32)
    gathered = jnp.sum(arrived, axis=0, keepdims=True)
    rows_q = displacement.shape[1]
    pairs_all = rows_q * nharm // 2
    rows = harm_idx * rows_q + jnp.arange(rows_q, dtype=jnp.int32)
    pair = (rows // 2).astype(jnp.float32)
    parity = (rows % 2).astype(jnp.float32)
    freq = 1.5 * (pair + 1.0) / pairs_all
    sign = 1.0 - 2.0 * parity
    disp = displacement.astype(jnp.float32)
    partner = disp.reshape(1, rows_q // 2, 2, width)[:, :, ::-1, :].reshape(1, rows_q, width)
    residual = (
        gathered
        - (freq * freq)[None, :, None] * lumped_mass[:, None, :] * disp
        + (sign * freq)[None, :, None] * damping[:, None, :] * partner
        - forcing
    )
    return (interior, residual, modes)


def solution(mesh):
    split = Mesh(
        mesh.devices.reshape(8, 8, 2, mesh.shape["harm"]), ("sub_0", "sub_1", "sub_2", "harm")
    )
    placed = (
        P(SUB),
        P(SUB, None),
        P(SUB, "harm", None),
        P(SUB, "harm", None),
        P(SUB, "harm", None),
        P(SUB, "harm", None),
        P(SUB, "harm", None),
        P(SUB, None),
        P(SUB, None),
    )
    return jax.shard_map(
        body,
        mesh=split,
        in_specs=placed,
        out_specs=(P(SUB, None, "harm"), P(SUB, "harm", None), P(SUB, "harm", None)),
        check_vma=False,
    )
```
